256 devices in a mesh: pb: 8 (over y, core), kv: 32 (over z, x).
Axes of the slice: x: 4, y: 4, z: 8, core: 2. Of those that a mesh axis runs over, the one named last changes fastest.
Arguments:
- queries: bfloat16 [65536, 4096], P(('pb', 'kv')), may hold values from -6 to 6
- keys: bfloat16 [8192, 4096], P(('pb', 'kv')), may hold values from -6 to 6
- values: bfloat16 [8192, 4096], P(('pb', 'kv')), may hold values from -6 to 6
- key_lists: int32 [512, 8], P('pb'), may hold values from 0 to 63, as said below
- counts: int32 [512], P('pb'), may hold values from 1 to 8, as said below
Outputs:
- attended: bfloat16 [65536, 4096], P(('pb', 'kv'))
The draws below stay inside these ranges and needn't reach their ends.
Inputs may be any that keep to these rules, and one draw needn't show every extreme that they name: For every query block the first counts entries of its row of key_lists name different key blocks; entries past counts are valid block numbers that do not take part. `counts`: some query block uses all 8 entries of its list.
All inputs are finite; a program needn't handle non-finite values.
Results may differ from the reference program's by a relative error of at most 0.011.
Values may be sent and summed in bfloat16 or wider, within the bound.
No kernel may reach another device: no remote copies, remote signals or barrier semaphores. Data moves between devices by JAX's collectives and lax.ppermute only.
A program may use at most 64 MiB of HBM per device.

```python
import jax
import jax.numpy as jnp
from jax import lax

HEADS = 32
HD = 128
BLK = 128
MOST = 8
QB_PB = 64
NQB = 512
NQ = 65536
NK = 8192
NKB = 64
WIDTH = 4096


def draw_queries(key, part):
    base = jax.random.fold_in(key, 11)
    field = jax.random.truncated_normal(base, -6.0, 6.0, (NQ, HEADS, HD), jnp.float32)
    return field.reshape(NQ, HEADS * HD).astype(jnp.bfloat16)


def draw_keys(key, part):
    base = jax.random.fold_in(key, 13)
    field = jax.random.truncated_normal(base, -6.0, 6.0, (NK, HEADS, HD), jnp.float32)
    return field.reshape(NK, HEADS * HD).astype(jnp.bfloat16)


def draw_key_lists(key, part):
    row_keys = jax.random.split(jax.random.fold_in(key, 17), NQB)
    chosen = jax.vmap(lambda row_key: jax.random.permutation(row_key, NKB)[:MOST])(row_keys)
    return chosen.astype(jnp.int32)


def draw_counts(key, part):
    first_key, second_key, third_key = jax.random.split(jax.random.fold_in(key, 19), 3)
    ceiling = jax.random.randint(first_key, (NQB // QB_PB,), 2, MOST + 1)
    ceiling_rows = jnp.repeat(ceiling, QB_PB)
    drawn = jax.random.randint(second_key, (NQB,), 0, 1048576) % ceiling_rows + 1
    fullest = jax.random.randint(third_key, (), 0, NQB)
    result = jnp.where(jnp.arange(NQB) == fullest, MOST, drawn)
    return result.astype(jnp.int32)


def block_levels(stream_key, shape, cuts, least, high):
    level, own = 1.0, jax.random.fold_in(stream_key, 6)
    for dim, parts in cuts:
        draws = jnp.exp(jax.random.uniform(jax.random.fold_in(own, dim), (parts,), jnp.float32, least / len(cuts), high / len(cuts)))
        level = level * jnp.repeat(draws, shape[dim] // parts).reshape([-1 if axis == dim else 1 for axis in range(len(shape))])
    return level


def scatter_about(rng, dims, width, bound, shards=(), dtype=jnp.bfloat16):
    values = jax.random.normal(rng, dims, jnp.float32) * width
    if len(shards) > 0:
        values = block_levels(rng, dims, shards, -0.22, 0.18) * values
    return jnp.clip(values, min=-bound, max=bound).astype(dtype)


def setup_inputs(seed: int = 0) -> dict:
    key_list = jax.random.split(jax.random.key(seed), 6)
    queries = draw_queries(jax.random.fold_in(key_list[5], 71), 0)
    keys = draw_keys(jax.random.fold_in(key_list[5], 71), 0)
    values = scatter_about(key_list[2], (NK, WIDTH), 1.0, 6.0, ((0, 256),))
    key_lists = draw_key_lists(jax.random.fold_in(key_list[5], 71), 0)
    counts = draw_counts(jax.random.fold_in(key_list[5], 71), 0)
    return {"queries": queries, "keys": keys, "values": values, "key_lists": key_lists, "counts": counts}


def reference(queries, keys, values, key_lists, counts):
    scaling = HD ** -0.5
    query_blocks = queries.reshape(NQB, BLK, HEADS, HD)
    key_blocks = keys.reshape(NKB, BLK, HEADS, HD)
    value_blocks = values.reshape(NKB, BLK, HEADS, HD)
    slot_of_key = jnp.arange(MOST * BLK) // BLK

    def single(item):
        block_queries, block_list, block_count = item
        listed_keys = key_blocks[block_list].reshape(MOST * BLK, HEADS, HD).astype(jnp.float32)
        listed_values = value_blocks[block_list].reshape(MOST * BLK, HEADS, HD).astype(jnp.float32)
        scores = jnp.einsum("qhd,khd->hqk", block_queries.astype(jnp.float32), listed_keys) * scaling
        usable = slot_of_key < block_count
        largest = jnp.max(jnp.where(usable, scores, -jnp.inf), axis=-1, keepdims=True)
        raised = jnp.where(usable, jnp.exp(scores - largest), 0.0)
        totals = jnp.sum(raised, axis=-1, keepdims=True)
        weights = (raised / totals).astype(jnp.bfloat16)
        output = jnp.einsum("hqk,khd->qhd", weights.astype(jnp.float32), listed_values)
        return output.astype(jnp.bfloat16).reshape(BLK, HEADS * HD)

    produced = lax.map(single, (query_blocks, key_lists, counts))
    return produced.reshape(NQ, HEADS * HD)
```

```python
import functools

import jax
import jax.numpy as jnp
from jax import lax
from jax.experimental import pallas as pl
from jax.experimental.pallas import tpu as pltpu
from jax.sharding import PartitionSpec as P

HEADS = 32
HD = 128
BLK = 128
MOST = 8


def attend_kernel(lists_ref, counts_ref, q_ref, kv_ref, o_ref, s_ref, m_ref, l_ref, acc_ref,
                  *, per_step, scaling):
    step = pl.program_id(1)

    def one(i, carry):
        qb = step * per_step + i
        cnt = counts_ref[qb]
        q = q_ref[i]
        m_ref[...] = jnp.full(m_ref.shape, -jnp.inf, jnp.float32)
        for s in range(MOST):
            @pl.when(s < cnt)
            def _():
                kb = lists_ref[qb * MOST + s]
                start = pl.multiple_of(kb * BLK, BLK)
                k = kv_ref[pl.ds(start, BLK), pl.ds(0, HD)]
                sc = lax.dot_general(q, k, (((1,), (1,)), ((), ())),
                                     preferred_element_type=jnp.float32) * scaling
                s_ref[s] = sc
                m_ref[...] = jnp.maximum(m_ref[...], jnp.max(sc, axis=-1, keepdims=True))

        l_ref[...] = jnp.zeros(l_ref.shape, jnp.float32)
        for s in range(MOST):
            @pl.when(s < cnt)
            def _():
                p = jnp.exp(s_ref[s] - m_ref[...])
                s_ref[s] = p
                l_ref[...] += jnp.sum(p, axis=-1, keepdims=True)

        acc_ref[...] = jnp.zeros(acc_ref.shape, jnp.float32)
        for s in range(MOST):
            @pl.when(s < cnt)
            def _():
                kb = lists_ref[qb * MOST + s]
                start = pl.multiple_of(kb * BLK, BLK)
                v = kv_ref[pl.ds(start, BLK), pl.ds(HD, HD)]
                w = (s_ref[s] / l_ref[...]).astype(jnp.bfloat16)
                acc_ref[...] += jnp.dot(w, v, preferred_element_type=jnp.float32)

        o_ref[i] = acc_ref[...].astype(o_ref.dtype)
        return carry

    lax.fori_loop(0, per_step, one, 0)


def attend(q_blocks, kv_rows, lists, counts, head_local):
    blocks = q_blocks.shape[0]
    per_step = 8 if blocks % 8 == 0 else 1
    nk = kv_rows.shape[0]
    kernel = functools.partial(attend_kernel, per_step=per_step, scaling=HD ** (-0.5))
    flops = blocks * head_local * MOST * 4 * BLK * BLK * HD
    grid_spec = pltpu.PrefetchScalarGridSpec(
        num_scalar_prefetch=2,
        grid=(head_local, blocks // per_step),
        in_specs=[
            pl.BlockSpec((per_step, BLK, HD), lambda h, b, *_: (b, 0, h)),
            pl.BlockSpec((nk, 2 * HD), lambda h, b, *_: (0, h)),
        ],
        out_specs=pl.BlockSpec((per_step, BLK, HD), lambda h, b, *_: (b, 0, h)),
        scratch_shapes=[
            pltpu.VMEM((MOST, BLK, BLK), jnp.float32),
            pltpu.VMEM((BLK, 1), jnp.float32),
            pltpu.VMEM((BLK, 1), jnp.float32),
            pltpu.VMEM((BLK, HD), jnp.float32),
        ],
    )
    return pl.pallas_call(
        kernel,
        grid_spec=grid_spec,
        out_shape=jax.ShapeDtypeStruct(q_blocks.shape, jnp.bfloat16),
        compiler_params=pltpu.CompilerParams(dimension_semantics=("arbitrary", "arbitrary")),
        cost_estimate=pl.CostEstimate(
            flops=flops,
            transcendentals=blocks * head_local * BLK * MOST * BLK,
            bytes_accessed=kv_rows.size * 2 + q_blocks.size * 4,
        ),
    )(lists.reshape(-1), counts, q_blocks, kv_rows)


def per_device(queries, keys, values, key_lists, counts):
    kv_count = lax.axis_size("kv")
    head_local = HEADS // kv_count
    tokens = keys.shape[0]
    stacked = jnp.stack(
        [keys.reshape(tokens, HEADS, HD), values.reshape(tokens, HEADS, HD)], axis=2
    )
    kv_split = lax.all_to_all(stacked, "kv", split_axis=1, concat_axis=0, tiled=True)
    kv_whole = lax.all_gather(kv_split, "pb", axis=0, tiled=True)
    kv_rows = kv_whole.reshape(kv_whole.shape[0], head_local * 2 * HD)

    query_blocks = queries.reshape(-1, BLK, queries.shape[1])
    exchanged = lax.all_to_all(query_blocks, "kv", split_axis=2, concat_axis=0, tiled=True)
    produced = attend(exchanged, kv_rows, key_lists, counts, head_local)
    result = lax.all_to_all(produced, "kv", split_axis=0, concat_axis=2, tiled=True)
    return result.reshape(queries.shape)


def solution(mesh):
    return jax.shard_map(
        per_device,
        mesh=mesh,
        in_specs=(
            P(("pb", "kv"), None),
            P(("pb", "kv"), None),
            P(("pb", "kv"), None),
            P("pb", None),
            P("pb"),
        ),
        out_specs=P(("pb", "kv"), None),
        check_vma=False,
    )
```

```python
import functools

import jax
import jax.numpy as jnp
from jax import lax
from jax.experimental import pallas as pl
from jax.experimental.pallas import tpu as pltpu
from jax.sharding import PartitionSpec as P

HEADS = 32
HD = 128
BLK = 128
MOST = 8


def attend_kernel(lists_ref, counts_ref, q_ref, kv_ref, o_ref, kc_ref, vc_ref, *, per_step, scaling):
    step = pl.program_id(1)

    def one(i, carry):
        qb = step * per_step + i
        cnt = counts_ref[qb]
        q = q_ref[i]
        for s in range(MOST):
            kb = lists_ref[qb * MOST + s]
            start = pl.multiple_of(kb * BLK, BLK)
            kc_ref[pl.ds(s * BLK, BLK), :] = kv_ref[pl.ds(start, BLK), pl.ds(0, HD)]
            vc_ref[pl.ds(s * BLK, BLK), :] = kv_ref[pl.ds(start, BLK), pl.ds(HD, HD)]
        sc = lax.dot_general(q, kc_ref[...], (((1,), (1,)), ((), ())),
                             preferred_element_type=jnp.float32) * scaling
        slot = lax.broadcasted_iota(jnp.int32, sc.shape, 1) // BLK
        sc = jnp.where(slot < cnt, sc, -jnp.inf)
        m = jnp.max(sc, axis=-1, keepdims=True)
        p = jnp.exp(sc - m)
        l = jnp.sum(p, axis=-1, keepdims=True)
        w = (p / l).astype(jnp.bfloat16)
        out = jnp.dot(w, vc_ref[...], preferred_element_type=jnp.float32)
        o_ref[i] = out.astype(o_ref.dtype)
        return carry

    lax.fori_loop(0, per_step, one, 0, unroll=2)


def attend(q_blocks, kv_rows, lists, counts, head_local):
    blocks = q_blocks.shape[0]
    per_step = 8 if blocks % 8 == 0 else 2
    nk = kv_rows.shape[0]
    kernel = functools.partial(attend_kernel, per_step=per_step, scaling=HD ** (-0.5))
    flops = blocks * head_local * MOST * 4 * BLK * BLK * HD
    grid_spec = pltpu.PrefetchScalarGridSpec(
        num_scalar_prefetch=2,
        grid=(head_local, blocks // per_step),
        in_specs=[
            pl.BlockSpec((per_step, BLK, HD), lambda h, b, *_: (b, 0, h)),
            pl.BlockSpec((nk, 2 * HD), lambda h, b, *_: (0, h)),
        ],
        out_specs=pl.BlockSpec((per_step, BLK, HD), lambda h, b, *_: (b, 0, h)),
        scratch_shapes=[
            pltpu.VMEM((MOST * BLK, HD), jnp.bfloat16),
            pltpu.VMEM((MOST * BLK, HD), jnp.bfloat16),
        ],
    )
    return pl.pallas_call(
        kernel,
        grid_spec=grid_spec,
        out_shape=jax.ShapeDtypeStruct(q_blocks.shape, jnp.bfloat16),
        compiler_params=pltpu.CompilerParams(dimension_semantics=("arbitrary", "arbitrary")),
        cost_estimate=pl.CostEstimate(
            flops=flops,
            transcendentals=blocks * head_local * BLK * MOST * BLK,
            bytes_accessed=kv_rows.size * 2 + q_blocks.size * 4,
        ),
    )(lists.reshape(-1), counts, q_blocks, kv_rows)


def per_device(queries, keys, values, key_lists, counts):
    kv_count = lax.axis_size("kv")
    head_local = HEADS // kv_count
    tokens = keys.shape[0]
    stacked = jnp.stack(
        [keys.reshape(tokens, HEADS, HD), values.reshape(tokens, HEADS, HD)], axis=2
    )
    kv_split = lax.all_to_all(stacked, "kv", split_axis=1, concat_axis=0, tiled=True)
    kv_whole = lax.all_gather(kv_split, "pb", axis=0, tiled=True)
    kv_rows = kv_whole.reshape(kv_whole.shape[0], head_local * 2 * HD)

    query_blocks = queries.reshape(-1, BLK, queries.shape[1])
    exchanged = lax.all_to_all(query_blocks, "kv", split_axis=2, concat_axis=0, tiled=True)
    produced = attend(exchanged, kv_rows, key_lists, counts, head_local)
    result = lax.all_to_all(produced, "kv", split_axis=0, concat_axis=2, tiled=True)
    return result.reshape(queries.shape)


def solution(mesh):
    return jax.shard_map(
        per_device,
        mesh=mesh,
        in_specs=(
            P(("pb", "kv"), None),
            P(("pb", "kv"), None),
            P(("pb", "kv"), None),
            P("pb", None),
            P("pb"),
        ),
        out_specs=P(("pb", "kv"), None),
        check_vma=False,
    )
```

```python
import functools

import jax
import jax.numpy as jnp
from jax import lax
from jax.experimental import pallas as pl
from jax.experimental.pallas import tpu as pltpu
from jax.sharding import PartitionSpec as P

HEADS = 32
HD = 128
BLK = 128
MOST = 8


def attend_kernel(lists_ref, counts_ref, q_ref, kv_ref, o_ref, kc_ref, vc_ref, *, per_step, scaling):
    step = pl.program_id(1)

    def one(i, carry):
        qb = step * per_step + i
        cnt = counts_ref[qb]
        q = q_ref[i]
        for s in range(MOST):
            kb = lists_ref[qb * MOST + s]
            start = pl.multiple_of(kb * BLK, BLK)
            kc_ref[pl.ds(s * BLK, BLK), :] = kv_ref[pl.ds(start, BLK), pl.ds(0, HD)]
            vc_ref[pl.ds(s * BLK, BLK), :] = kv_ref[pl.ds(start, BLK), pl.ds(HD, HD)]
        sc = lax.dot_general(q, kc_ref[...], (((1,), (1,)), ((), ())),
                             preferred_element_type=jnp.float32) * scaling
        slot = lax.broadcasted_iota(jnp.int32, sc.shape, 1) // BLK
        sc = jnp.where(slot < cnt, sc, -jnp.inf)
        m = jnp.max(sc, axis=-1, keepdims=True)
        p = jnp.exp(sc - m)
        l = jnp.sum(p, axis=-1, keepdims=True)
        w = (p / l).astype(jnp.bfloat16)
        out = jnp.dot(w, vc_ref[...], preferred_element_type=jnp.float32)
        o_ref[i] = out.astype(o_ref.dtype)
        return carry

    lax.fori_loop(0, per_step, one, 0, unroll=2)


def attend(q_blocks, kv_rows, lists, counts, head_local):
    blocks = q_blocks.shape[0]
    per_step = 8 if blocks % 8 == 0 else 2
    nk = kv_rows.shape[0]
    kernel = functools.partial(attend_kernel, per_step=per_step, scaling=HD ** (-0.5))
    flops = blocks * head_local * MOST * 4 * BLK * BLK * HD
    grid_spec = pltpu.PrefetchScalarGridSpec(
        num_scalar_prefetch=2,
        grid=(head_local, blocks // per_step),
        in_specs=[
            pl.BlockSpec((per_step, BLK, HD), lambda h, b, *_: (b, 0, h)),
            pl.BlockSpec((nk, 2 * HD), lambda h, b, *_: (0, h)),
        ],
        out_specs=pl.BlockSpec((per_step, BLK, HD), lambda h, b, *_: (b, 0, h)),
        scratch_shapes=[
            pltpu.VMEM((MOST * BLK, HD), jnp.bfloat16),
            pltpu.VMEM((MOST * BLK, HD), jnp.bfloat16),
        ],
    )
    return pl.pallas_call(
        kernel,
        grid_spec=grid_spec,
        out_shape=jax.ShapeDtypeStruct(q_blocks.shape, jnp.bfloat16),
        compiler_params=pltpu.CompilerParams(dimension_semantics=("arbitrary", "arbitrary")),
        cost_estimate=pl.CostEstimate(
            flops=flops,
            transcendentals=blocks * head_local * BLK * MOST * BLK,
            bytes_accessed=kv_rows.size * 2 + q_blocks.size * 4,
        ),
    )(lists.reshape(-1), counts, q_blocks, kv_rows)


def per_device(queries, keys, values, key_lists, counts, *, x_count):
    group = ("y", "core", "x")
    pb_count = lax.axis_size("y") * lax.axis_size("core")
    z_count = lax.axis_size("z")
    group_count = pb_count * x_count
    kv_count = z_count * x_count
    head_local = HEADS // group_count
    tokens = keys.shape[0]
    assert BLK == x_count * tokens
    stacked = jnp.stack(
        [keys.reshape(tokens, HEADS, HD), values.reshape(tokens, HEADS, HD)], axis=2
    )
    kv_split = lax.all_to_all(stacked, group, split_axis=1, concat_axis=0, tiled=True)
    kv_whole = lax.all_gather(kv_split, "z", axis=0, tiled=True)
    kv_rows = kv_whole.reshape(kv_whole.shape[0], head_local * 2 * HD)

    all_lists = lax.all_gather(key_lists, ("y", "core"), axis=0, tiled=True)
    all_counts = lax.all_gather(counts, ("y", "core"), axis=0, tiled=True)
    per_dev = queries.shape[0] // BLK
    member = jnp.arange(group_count, dtype=jnp.int32)
    first = ((member // x_count) * kv_count + member % x_count) * per_dev
    ids = (first[:, None] + jnp.arange(per_dev, dtype=jnp.int32)[None, :]).reshape(-1)
    ids = ids + lax.axis_index("z") * (x_count * per_dev)
    lists = all_lists[ids]
    lists = (lists % z_count) * pb_count + lists // z_count
    local_counts = all_counts[ids]

    query_blocks = queries.reshape(-1, BLK, queries.shape[1])
    exchanged = lax.all_to_all(query_blocks, group, split_axis=2, concat_axis=0, tiled=True)
    produced = attend(exchanged, kv_rows, lists, local_counts, head_local)
    result = lax.all_to_all(produced, group, split_axis=0, concat_axis=2, tiled=True)
    return result.reshape(queries.shape)


def solution(mesh):
    pb_count, kv_count = mesh.shape["pb"], mesh.shape["kv"]
    x_count = 4
    fine = jax.sharding.Mesh(
        mesh.devices.reshape(pb_count // 2, 2, kv_count // x_count, x_count),
        ("y", "core", "z", "x"),
    )
    rows = P(("y", "core", "z", "x"), None)
    return jax.shard_map(
        functools.partial(per_device, x_count=x_count),
        mesh=fine,
        in_specs=(rows, rows, rows, P(("y", "core"), None), P(("y", "core"))),
        out_specs=rows,
        check_vma=False,
    )
```

```python
import functools

import jax
import jax.numpy as jnp
from jax import lax
from jax.experimental import pallas as pl
from jax.experimental.pallas import tpu as pltpu
from jax.sharding import PartitionSpec as P

HEADS = 32
HD = 128
BLK = 128
MOST = 8


def attend_kernel(lists_ref, counts_ref, q_ref, kv_ref, o_ref, kc_ref, vc_ref, *, per_step, scaling):
    step = pl.program_id(1)

    def one(i, carry):
        qb = step * per_step + i
        cnt = counts_ref[qb]
        q = q_ref[i]
        for s in range(MOST):
            kb = lists_ref[qb * MOST + s]
            start = pl.multiple_of(kb * BLK, BLK)
            kc_ref[pl.ds(s * BLK, BLK), :] = kv_ref[pl.ds(start, BLK), pl.ds(0, HD)]
            vc_ref[pl.ds(s * BLK, BLK), :] = kv_ref[pl.ds(start, BLK), pl.ds(HD, HD)]
        sc = lax.dot_general(q, kc_ref[...], (((1,), (1,)), ((), ())),
                             preferred_element_type=jnp.float32) * scaling
        slot = lax.broadcasted_iota(jnp.int32, sc.shape, 1) // BLK
        sc = jnp.where(slot < cnt, sc, -jnp.inf)
        m = jnp.max(sc, axis=-1, keepdims=True)
        p = jnp.exp(sc - m)
        l = jnp.sum(p, axis=-1, keepdims=True)
        w = (p / l).astype(jnp.bfloat16)
        out = jnp.dot(w, vc_ref[...], preferred_element_type=jnp.float32)
        o_ref[i] = out.astype(o_ref.dtype)
        return carry

    lax.fori_loop(0, per_step, one, 0, unroll=2)


def attend(q_blocks, kv_rows, lists, counts, head_local):
    blocks = q_blocks.shape[0]
    per_step = 8 if blocks % 8 == 0 else 2
    nk = kv_rows.shape[0]
    kernel = functools.partial(attend_kernel, per_step=per_step, scaling=HD ** (-0.5))
    flops = blocks * head_local * MOST * 4 * BLK * BLK * HD
    grid_spec = pltpu.PrefetchScalarGridSpec(
        num_scalar_prefetch=2,
        grid=(head_local, blocks // per_step),
        in_specs=[
            pl.BlockSpec((per_step, BLK, HD), lambda h, b, *_: (b, 0, h)),
            pl.BlockSpec((nk, 2 * HD), lambda h, b, *_: (0, h)),
        ],
        out_specs=pl.BlockSpec((per_step, BLK, HD), lambda h, b, *_: (b, 0, h)),
        scratch_shapes=[
            pltpu.VMEM((MOST * BLK, HD), jnp.bfloat16),
            pltpu.VMEM((MOST * BLK, HD), jnp.bfloat16),
        ],
    )
    return pl.pallas_call(
        kernel,
        grid_spec=grid_spec,
        out_shape=jax.ShapeDtypeStruct(q_blocks.shape, jnp.bfloat16),
        compiler_params=pltpu.CompilerParams(dimension_semantics=("arbitrary", "arbitrary")),
        cost_estimate=pl.CostEstimate(
            flops=flops,
            transcendentals=blocks * head_local * BLK * MOST * BLK,
            bytes_accessed=kv_rows.size * 2 + q_blocks.size * 4,
        ),
    )(lists.reshape(-1), counts, q_blocks, kv_rows)


def per_device(queries, keys, values, key_lists, counts, *, x_count):
    group = ("y", "core", "x")
    pb_count = lax.axis_size("y") * lax.axis_size("core")
    z_count = lax.axis_size("z")
    group_count = pb_count * x_count
    kv_count = z_count * x_count
    head_local = HEADS // group_count
    tokens = keys.shape[0]
    assert BLK == x_count * tokens
    per_dev = queries.shape[0] // BLK
    meta_width = per_dev * (MOST + 1)
    assert meta_width <= 2 * HD
    kv_index = lax.axis_index("z") * x_count + lax.axis_index("x")
    own_lists = lax.dynamic_slice_in_dim(key_lists, kv_index * per_dev, per_dev, axis=0)
    own_counts = lax.dynamic_slice_in_dim(counts, kv_index * per_dev, per_dev, axis=0)
    meta = jnp.concatenate([own_lists, own_counts[:, None]], axis=1).reshape(-1)
    meta_row = jnp.zeros((2 * HD,), jnp.bfloat16).at[:meta_width].set(meta.astype(jnp.bfloat16))
    meta_token = jnp.broadcast_to(meta_row.reshape(1, 1, 2, HD), (1, HEADS, 2, HD))
    stacked = jnp.concatenate(
        [
            jnp.stack(
                [keys.reshape(tokens, HEADS, HD), values.reshape(tokens, HEADS, HD)], axis=2
            ),
            meta_token,
        ],
        axis=0,
    )
    kv_split = lax.all_to_all(stacked, group, split_axis=1, concat_axis=0, tiled=True)
    kv_split = kv_split.reshape(group_count, tokens + 1, head_local, 2, HD)
    kv_part = kv_split[:, :tokens].reshape(group_count * tokens, head_local, 2, HD)
    kv_whole = lax.all_gather(kv_part, "z", axis=0, tiled=True)
    kv_rows = kv_whole.reshape(kv_whole.shape[0], head_local * 2 * HD)

    meta_in = kv_split[:, tokens, 0].reshape(group_count, 2 * HD)[:, :meta_width]
    meta_in = meta_in.astype(jnp.int32).reshape(group_count * per_dev, MOST + 1)
    lists = meta_in[:, :MOST]
    lists = (lists % z_count) * pb_count + lists // z_count
    local_counts = meta_in[:, MOST]

    query_blocks = queries.reshape(-1, BLK, queries.shape[1])
    exchanged = lax.all_to_all(query_blocks, group, split_axis=2, concat_axis=0, tiled=True)
    produced = attend(exchanged, kv_rows, lists, local_counts, head_local)
    result = lax.all_to_all(produced, group, split_axis=0, concat_axis=2, tiled=True)
    return result.reshape(queries.shape)


def solution(mesh):
    pb_count, kv_count = mesh.shape["pb"], mesh.shape["kv"]
    x_count = 4
    fine = jax.sharding.Mesh(
        mesh.devices.reshape(pb_count // 2, 2, kv_count // x_count, x_count),
        ("y", "core", "z", "x"),
    )
    rows = P(("y", "core", "z", "x"), None)
    return jax.shard_map(
        functools.partial(per_device, x_count=x_count),
        mesh=fine,
        in_specs=(rows, rows, rows, P(("y", "core"), None), P(("y", "core"))),
        out_specs=rows,
        check_vma=False,
    )
```

```python
import functools

import jax
import jax.numpy as jnp
from jax import lax
from jax.experimental import pallas as pl
from jax.experimental.pallas import tpu as pltpu
from jax.sharding import PartitionSpec as P

HEADS = 32
HD = 128
BLK = 128
MOST = 8


def attend_kernel(lists_ref, counts_ref, q_ref, kv_ref, o_ref, kc_ref, vc_ref,
                  *, per_step, per_dev, scaling):
    step = pl.program_id(1)
    for i in range(per_step):
        qb = step * per_step + i
        cnt = counts_ref[qb]
        q = q_ref[i // per_dev, pl.ds((i % per_dev) * BLK, BLK), :]
        for s in range(MOST):
            kb = lists_ref[qb * MOST + s]
            start = pl.multiple_of(kb * BLK, BLK)
            kc_ref[pl.ds(s * BLK, BLK), :] = kv_ref[pl.ds(start, BLK), pl.ds(0, HD)]
            vc_ref[pl.ds(s * BLK, BLK), :] = kv_ref[pl.ds(start, BLK), pl.ds(HD, HD)]
        sc = lax.dot_general(q, kc_ref[...], (((1,), (1,)), ((), ())),
                             preferred_element_type=jnp.float32) * scaling
        slot = lax.broadcasted_iota(jnp.int32, sc.shape, 1) // BLK
        sc = jnp.where(slot < cnt, sc, -jnp.inf)
        m = jnp.max(sc, axis=-1, keepdims=True)
        p = jnp.exp(sc - m)
        l = jnp.sum(p, axis=-1, keepdims=True)
        w = (p / l).astype(jnp.bfloat16)
        out = jnp.dot(w, vc_ref[...], preferred_element_type=jnp.float32)
        o_ref[i] = out.astype(o_ref.dtype)


def attend(q_src, kv_rows, lists, counts, per_dev):
    sources = q_src.shape[0]
    blocks = sources * per_dev
    per_src = 4 if sources % 4 == 0 else 1
    per_step = per_src * per_dev
    nk = kv_rows.shape[0]
    kernel = functools.partial(
        attend_kernel, per_step=per_step, per_dev=per_dev, scaling=HD ** (-0.5)
    )
    flops = blocks * MOST * 4 * BLK * BLK * HD
    grid_spec = pltpu.PrefetchScalarGridSpec(
        num_scalar_prefetch=2,
        grid=(1, blocks // per_step),
        in_specs=[
            pl.BlockSpec((per_src, per_dev * BLK, HD), lambda h, b, *_: (b, 0, h)),
            pl.BlockSpec((nk, 2 * HD), lambda h, b, *_: (0, h)),
        ],
        out_specs=pl.BlockSpec((per_step, BLK, HD), lambda h, b, *_: (b, 0, h)),
        scratch_shapes=[
            pltpu.VMEM((MOST * BLK, HD), jnp.bfloat16),
            pltpu.VMEM((MOST * BLK, HD), jnp.bfloat16),
        ],
    )
    return pl.pallas_call(
        kernel,
        grid_spec=grid_spec,
        out_shape=jax.ShapeDtypeStruct((blocks, BLK, HD), jnp.bfloat16),
        compiler_params=pltpu.CompilerParams(dimension_semantics=("arbitrary", "arbitrary")),
        cost_estimate=pl.CostEstimate(
            flops=flops,
            transcendentals=blocks * BLK * MOST * BLK,
            bytes_accessed=kv_rows.size * 2 + blocks * BLK * HD * 4,
        ),
    )(lists.reshape(-1), counts, q_src, kv_rows)


def per_device(queries, keys, values, key_lists, counts, *, x_count):
    group = ("y", "core", "x")
    pb_count = lax.axis_size("y") * lax.axis_size("core")
    z_count = lax.axis_size("z")
    group_count = pb_count * x_count
    kv_count = z_count * x_count
    assert HEADS == group_count
    tokens = keys.shape[0]
    assert BLK == x_count * tokens
    rows = queries.shape[0]
    per_dev = rows // BLK
    meta_width = per_dev * (MOST + 1)
    meta_rows = 16
    assert meta_width <= HD

    kv_heads = jnp.concatenate(
        [
            keys.reshape(tokens, HEADS, HD).transpose(1, 0, 2),
            values.reshape(tokens, HEADS, HD).transpose(1, 0, 2),
        ],
        axis=2,
    )
    kv_split = lax.all_to_all(kv_heads, group, split_axis=0, concat_axis=0, tiled=True)
    kv_part = kv_split.reshape(group_count * tokens, 2 * HD)
    kv_rows = lax.all_gather(kv_part, "z", axis=0, tiled=True)

    kv_index = lax.axis_index("z") * x_count + lax.axis_index("x")
    own_lists = lax.dynamic_slice_in_dim(key_lists, kv_index * per_dev, per_dev, axis=0)
    own_counts = lax.dynamic_slice_in_dim(counts, kv_index * per_dev, per_dev, axis=0)
    meta = jnp.concatenate([own_lists, own_counts[:, None]], axis=1).reshape(-1)
    meta_block = jnp.zeros((meta_rows, HD), jnp.bfloat16).at[0, :meta_width].set(
        meta.astype(jnp.bfloat16)
    )
    q_heads = jnp.concatenate(
        [
            queries.reshape(rows, HEADS, HD).transpose(1, 0, 2),
            jnp.broadcast_to(meta_block[None], (HEADS, meta_rows, HD)),
        ],
        axis=1,
    )
    q_src = lax.all_to_all(q_heads, group, split_axis=0, concat_axis=0, tiled=True)

    meta_in = q_src[:, rows, :meta_width].astype(jnp.int32)
    meta_in = meta_in.reshape(group_count * per_dev, MOST + 1)
    lists = meta_in[:, :MOST]
    lists = (lists % z_count) * pb_count + lists // z_count
    local_counts = meta_in[:, MOST]

    produced = attend(q_src, kv_rows, lists, local_counts, per_dev)
    back = lax.all_to_all(
        produced.reshape(group_count, rows, HD), group, split_axis=0, concat_axis=0, tiled=True
    )
    return back.transpose(1, 0, 2).reshape(queries.shape)


def solution(mesh):
    pb_count, kv_count = mesh.shape["pb"], mesh.shape["kv"]
    x_count = 4
    fine = jax.sharding.Mesh(
        mesh.devices.reshape(pb_count // 2, 2, kv_count // x_count, x_count),
        ("y", "core", "z", "x"),
    )
    rows = P(("y", "core", "z", "x"), None)
    return jax.shard_map(
        functools.partial(per_device, x_count=x_count),
        mesh=fine,
        in_specs=(rows, rows, rows, P(("y", "core"), None), P(("y", "core"))),
        out_specs=rows,
        check_vma=False,
    )
```

```python
import functools

import jax
import jax.numpy as jnp
from jax import lax
from jax.experimental import pallas as pl
from jax.experimental.pallas import tpu as pltpu
from jax.sharding import PartitionSpec as P

HEADS = 32
HD = 128
BLK = 128
MOST = 8


def attend_kernel(lists_ref, counts_ref, q_ref, kv_ref, o_ref, kc_ref, vc_ref,
                  *, per_step, scaling):
    step = pl.program_id(1)
    for i in range(per_step):
        qb = step * per_step + i
        cnt = counts_ref[qb]
        q = q_ref[i]
        for s in range(MOST):
            kb = lists_ref[qb * MOST + s]
            start = pl.multiple_of(kb * BLK, BLK)
            kc_ref[pl.ds(s * BLK, BLK), :] = kv_ref[pl.ds(start, BLK), pl.ds(0, HD)]
            vc_ref[pl.ds(s * BLK, BLK), :] = kv_ref[pl.ds(start, BLK), pl.ds(HD, HD)]
        sc = lax.dot_general(q, kc_ref[...], (((1,), (1,)), ((), ())),
                             preferred_element_type=jnp.float32) * scaling
        slot = lax.broadcasted_iota(jnp.int32, sc.shape, 1) // BLK
        sc = jnp.where(slot < cnt, sc, -jnp.inf)
        m = jnp.max(sc, axis=-1, keepdims=True)
        p = jnp.exp(sc - m)
        l = jnp.sum(p, axis=-1, keepdims=True)
        w = (p / l).astype(jnp.bfloat16)
        out = jnp.dot(w, vc_ref[...], preferred_element_type=jnp.float32)
        o_ref[i] = out.astype(o_ref.dtype)


def attend(q_src, kv_rows, lists, counts, half):
    blocks = q_src.shape[0]
    per_step = 8 if blocks % 8 == 0 else 1
    nk = kv_rows.shape[0]
    kernel = functools.partial(attend_kernel, per_step=per_step, scaling=HD ** (-0.5))
    flops = blocks * MOST * 4 * BLK * BLK * HD
    grid_spec = pltpu.PrefetchScalarGridSpec(
        num_scalar_prefetch=2,
        grid=(1, blocks // per_step),
        in_specs=[
            pl.BlockSpec((per_step, BLK, HD), lambda h, b, *_: (b, half, h)),
            pl.BlockSpec((nk, 2 * HD), lambda h, b, *_: (0, h)),
        ],
        out_specs=pl.BlockSpec((per_step, BLK, HD), lambda h, b, *_: (b, 0, h)),
        scratch_shapes=[
            pltpu.VMEM((MOST * BLK, HD), jnp.bfloat16),
            pltpu.VMEM((MOST * BLK, HD), jnp.bfloat16),
        ],
    )
    return pl.pallas_call(
        kernel,
        grid_spec=grid_spec,
        out_shape=jax.ShapeDtypeStruct((blocks, BLK, HD), jnp.bfloat16),
        compiler_params=pltpu.CompilerParams(dimension_semantics=("arbitrary", "arbitrary")),
        cost_estimate=pl.CostEstimate(
            flops=flops,
            transcendentals=blocks * BLK * MOST * BLK,
            bytes_accessed=kv_rows.size * 2 + blocks * BLK * HD * 4,
        ),
    )(lists.reshape(-1), counts, q_src, kv_rows)


def per_device(queries, keys, values, key_lists, counts, *, x_count):
    group = ("y", "core", "x")
    pb_count = lax.axis_size("y") * lax.axis_size("core")
    z_count = lax.axis_size("z")
    group_count = pb_count * x_count
    kv_count = z_count * x_count
    assert HEADS == group_count
    tokens = keys.shape[0]
    assert BLK == x_count * tokens
    rows = queries.shape[0]
    per_dev = rows // BLK
    meta_width = per_dev * (MOST + 1)
    meta_rows = 16
    assert meta_width <= HD

    kv_heads = jnp.concatenate(
        [
            keys.reshape(tokens, HEADS, HD).transpose(1, 0, 2),
            values.reshape(tokens, HEADS, HD).transpose(1, 0, 2),
        ],
        axis=2,
    )
    kv_split = lax.all_to_all(kv_heads, group, split_axis=0, concat_axis=0, tiled=True)
    kv_part = kv_split.reshape(group_count * tokens, 2 * HD)
    kv_rows = lax.all_gather(kv_part, "z", axis=0, tiled=True)

    kv_index = lax.axis_index("z") * x_count + lax.axis_index("x")
    own_lists = lax.dynamic_slice_in_dim(key_lists, kv_index * per_dev, per_dev, axis=0)
    own_counts = lax.dynamic_slice_in_dim(counts, kv_index * per_dev, per_dev, axis=0)
    meta = jnp.concatenate([own_lists, own_counts[:, None]], axis=1).reshape(-1)
    meta_block = jnp.zeros((meta_rows, HD), jnp.bfloat16).at[0, :meta_width].set(
        meta.astype(jnp.bfloat16)
    )
    q_heads = jnp.concatenate(
        [
            queries.reshape(rows, HEADS, HD).transpose(1, 0, 2),
            jnp.broadcast_to(meta_block[None], (HEADS, meta_rows, HD)),
        ],
        axis=1,
    )
    q_src = lax.all_to_all(q_heads, group, split_axis=0, concat_axis=0, tiled=True)

    meta_in = q_src[:, rows, :meta_width].astype(jnp.int32)
    meta_in = meta_in.reshape(group_count * per_dev, MOST + 1)
    lists = meta_in[:, :MOST]
    lists = (lists % z_count) * pb_count + lists // z_count
    local_counts = meta_in[:, MOST]

    lists = lists.reshape(group_count, per_dev, MOST)
    local_counts = local_counts.reshape(group_count, per_dev)
    halves = []
    for t in range(per_dev):
        part = attend(q_src, kv_rows, lists[:, t], local_counts[:, t], t)
        halves.append(lax.all_to_all(part, group, split_axis=0, concat_axis=0, tiled=True))
    back = jnp.concatenate(
        [half.transpose(1, 0, 2).reshape(BLK, HEADS * HD) for half in halves], axis=0
    )
    return back.reshape(queries.shape)


def solution(mesh):
    pb_count, kv_count = mesh.shape["pb"], mesh.shape["kv"]
    x_count = 4
    fine = jax.sharding.Mesh(
        mesh.devices.reshape(pb_count // 2, 2, kv_count // x_count, x_count),
        ("y", "core", "z", "x"),
    )
    rows = P(("y", "core", "z", "x"), None)
    return jax.shard_map(
        functools.partial(per_device, x_count=x_count),
        mesh=fine,
        in_specs=(rows, rows, rows, P(("y", "core"), None), P(("y", "core"))),
        out_specs=rows,
        check_vma=False,
    )
```

```python
import functools

import jax
import jax.numpy as jnp
from jax import lax
from jax.experimental import pallas as pl
from jax.experimental.pallas import tpu as pltpu
from jax.sharding import PartitionSpec as P

HEADS = 32
HD = 128
BLK = 128
MOST = 8


SLOT_SIZES = (2, 4, MOST)


def attend_kernel(step_ref, lists_ref, counts_ref, q_ref, kv_ref, o_ref, kc_ref, vc_ref,
                  *, per_step, per_dev, scaling):
    step = pl.program_id(1)

    def body_for(slots):
        def body():
            for i in range(per_step):
                qb = step * per_step + i
                cnt = counts_ref[qb]
                q = q_ref[i // per_dev, pl.ds((i % per_dev) * BLK, BLK), :]
                for s in range(slots):
                    kb = lists_ref[qb * MOST + s]
                    start = pl.multiple_of(kb * BLK, BLK)
                    kc_ref[pl.ds(s * BLK, BLK), :] = kv_ref[pl.ds(start, BLK), pl.ds(0, HD)]
                    vc_ref[pl.ds(s * BLK, BLK), :] = kv_ref[pl.ds(start, BLK), pl.ds(HD, HD)]
                sc = lax.dot_general(q, kc_ref[pl.ds(0, slots * BLK), :], (((1,), (1,)), ((), ())),
                                     preferred_element_type=jnp.float32) * scaling
                slot = lax.broadcasted_iota(jnp.int32, sc.shape, 1) // BLK
                sc = jnp.where(slot < cnt, sc, -jnp.inf)
                m = jnp.max(sc, axis=-1, keepdims=True)
                p = jnp.exp(sc - m)
                l = jnp.sum(p, axis=-1, keepdims=True)
                w = (p / l).astype(jnp.bfloat16)
                out = jnp.dot(w, vc_ref[pl.ds(0, slots * BLK), :],
                              preferred_element_type=jnp.float32)
                o_ref[i] = out.astype(o_ref.dtype)
        return body

    lax.switch(step_ref[step], [body_for(n) for n in SLOT_SIZES])


def attend(q_src, kv_rows, lists, counts, per_dev):
    sources = q_src.shape[0]
    blocks = sources * per_dev
    per_src = 4 if sources % 4 == 0 else 1
    per_step = per_src * per_dev
    nk = kv_rows.shape[0]
    kernel = functools.partial(
        attend_kernel, per_step=per_step, per_dev=per_dev, scaling=HD ** (-0.5)
    )
    flops = blocks * MOST * 4 * BLK * BLK * HD
    widest = jnp.max(counts.reshape(blocks // per_step, per_step), axis=1)
    step_size = jnp.zeros_like(widest)
    for n in SLOT_SIZES[:-1]:
        step_size = step_size + (widest > n).astype(jnp.int32)
    grid_spec = pltpu.PrefetchScalarGridSpec(
        num_scalar_prefetch=3,
        grid=(1, blocks // per_step),
        in_specs=[
            pl.BlockSpec((per_src, per_dev * BLK, HD), lambda h, b, *_: (b, 0, h)),
            pl.BlockSpec((nk, 2 * HD), lambda h, b, *_: (0, h)),
        ],
        out_specs=pl.BlockSpec((per_step, BLK, HD), lambda h, b, *_: (b, 0, h)),
        scratch_shapes=[
            pltpu.VMEM((MOST * BLK, HD), jnp.bfloat16),
            pltpu.VMEM((MOST * BLK, HD), jnp.bfloat16),
        ],
    )
    return pl.pallas_call(
        kernel,
        grid_spec=grid_spec,
        out_shape=jax.ShapeDtypeStruct((blocks, BLK, HD), jnp.bfloat16),
        compiler_params=pltpu.CompilerParams(dimension_semantics=("arbitrary", "arbitrary")),
        cost_estimate=pl.CostEstimate(
            flops=flops,
            transcendentals=blocks * BLK * MOST * BLK,
            bytes_accessed=kv_rows.size * 2 + blocks * BLK * HD * 4,
        ),
    )(step_size, lists.reshape(-1), counts, q_src, kv_rows)


def per_device(queries, keys, values, key_lists, counts, *, x_count):
    group = ("y", "core", "x")
    pb_count = lax.axis_size("y") * lax.axis_size("core")
    z_count = lax.axis_size("z")
    group_count = pb_count * x_count
    kv_count = z_count * x_count
    assert HEADS == group_count
    tokens = keys.shape[0]
    assert BLK == x_count * tokens
    rows = queries.shape[0]
    per_dev = rows // BLK
    meta_width = per_dev * (MOST + 1)
    meta_rows = 16
    assert meta_width <= HD

    kv_heads = jnp.concatenate(
        [
            keys.reshape(tokens, HEADS, HD).transpose(1, 0, 2),
            values.reshape(tokens, HEADS, HD).transpose(1, 0, 2),
        ],
        axis=2,
    )
    kv_split = lax.all_to_all(kv_heads, group, split_axis=0, concat_axis=0, tiled=True)
    kv_part = kv_split.reshape(group_count * tokens, 2 * HD)
    kv_rows = lax.all_gather(kv_part, "z", axis=0, tiled=True)

    kv_index = lax.axis_index("z") * x_count + lax.axis_index("x")
    own_lists = lax.dynamic_slice_in_dim(key_lists, kv_index * per_dev, per_dev, axis=0)
    own_counts = lax.dynamic_slice_in_dim(counts, kv_index * per_dev, per_dev, axis=0)
    meta = jnp.concatenate([own_lists, own_counts[:, None]], axis=1).reshape(-1)
    meta_block = jnp.zeros((meta_rows, HD), jnp.bfloat16).at[0, :meta_width].set(
        meta.astype(jnp.bfloat16)
    )
    q_heads = jnp.concatenate(
        [
            queries.reshape(rows, HEADS, HD).transpose(1, 0, 2),
            jnp.broadcast_to(meta_block[None], (HEADS, meta_rows, HD)),
        ],
        axis=1,
    )
    q_src = lax.all_to_all(q_heads, group, split_axis=0, concat_axis=0, tiled=True)

    meta_in = q_src[:, rows, :meta_width].astype(jnp.int32)
    meta_in = meta_in.reshape(group_count * per_dev, MOST + 1)
    lists = meta_in[:, :MOST]
    lists = (lists % z_count) * pb_count + lists // z_count
    local_counts = meta_in[:, MOST]

    produced = attend(q_src, kv_rows, lists, local_counts, per_dev)
    back = lax.all_to_all(
        produced.reshape(group_count, rows, HD), group, split_axis=0, concat_axis=0, tiled=True
    )
    return back.transpose(1, 0, 2).reshape(queries.shape)


def solution(mesh):
    pb_count, kv_count = mesh.shape["pb"], mesh.shape["kv"]
    x_count = 4
    fine = jax.sharding.Mesh(
        mesh.devices.reshape(pb_count // 2, 2, kv_count // x_count, x_count),
        ("y", "core", "z", "x"),
    )
    rows = P(("y", "core", "z", "x"), None)
    return jax.shard_map(
        functools.partial(per_device, x_count=x_count),
        mesh=fine,
        in_specs=(rows, rows, rows, P(("y", "core"), None), P(("y", "core"))),
        out_specs=rows,
        check_vma=False,
    )
```

```python
import functools

import jax
import jax.numpy as jnp
from jax import lax
from jax.experimental import pallas as pl
from jax.experimental.pallas import tpu as pltpu
from jax.sharding import PartitionSpec as P

HEADS = 32
HD = 128
BLK = 128
MOST = 8


SLOT_SIZES = (2, 4, MOST)


def weights_kernel(step_ref, lists_ref, counts_ref, q_ref, k_ref, w_ref, kc_ref,
                   *, per_step, per_dev, scaling):
    step = pl.program_id(0)

    def body_for(slots):
        def body():
            for i in range(per_step):
                qb = step * per_step + i
                cnt = counts_ref[qb]
                q = q_ref[i // per_dev, pl.ds((i % per_dev) * BLK, BLK), :]
                for s in range(slots):
                    kb = lists_ref[qb * MOST + s]
                    start = pl.multiple_of(kb * BLK, BLK)
                    kc_ref[pl.ds(s * BLK, BLK), :] = k_ref[pl.ds(start, BLK), :]
                sc = lax.dot_general(q, kc_ref[pl.ds(0, slots * BLK), :], (((1,), (1,)), ((), ())),
                                     preferred_element_type=jnp.float32) * scaling
                slot = lax.broadcasted_iota(jnp.int32, sc.shape, 1) // BLK
                sc = jnp.where(slot < cnt, sc, -jnp.inf)
                m = jnp.max(sc, axis=-1, keepdims=True)
                p = jnp.exp(sc - m)
                l = jnp.sum(p, axis=-1, keepdims=True)
                w_ref[i, :, pl.ds(0, slots * BLK)] = (p / l).astype(jnp.bfloat16)
        return body

    lax.switch(step_ref[step], [body_for(n) for n in SLOT_SIZES])


def mix_kernel(step_ref, lists_ref, w_ref, v_ref, o_ref, vc_ref, *, per_step):
    step = pl.program_id(0)

    def body_for(slots):
        def body():
            for i in range(per_step):
                qb = step * per_step + i
                for s in range(slots):
                    kb = lists_ref[qb * MOST + s]
                    start = pl.multiple_of(kb * BLK, BLK)
                    vc_ref[pl.ds(s * BLK, BLK), :] = v_ref[pl.ds(start, BLK), :]
                w = w_ref[i, :, pl.ds(0, slots * BLK)]
                out = jnp.dot(w, vc_ref[pl.ds(0, slots * BLK), :],
                              preferred_element_type=jnp.float32)
                o_ref[i] = out.astype(o_ref.dtype)
        return body

    lax.switch(step_ref[step], [body_for(n) for n in SLOT_SIZES])


def attend(q_src, k_rows, v_rows, lists, counts, per_dev, order_after=None):
    sources = q_src.shape[0]
    blocks = sources * per_dev
    per_src = 4 if sources % 4 == 0 else 1
    per_step = per_src * per_dev
    nk = k_rows.shape[0]
    width = MOST * BLK
    widest = jnp.max(counts.reshape(blocks // per_step, per_step), axis=1)
    step_size = jnp.zeros_like(widest)
    for n in SLOT_SIZES[:-1]:
        step_size = step_size + (widest > n).astype(jnp.int32)
    flat_lists = lists.reshape(-1)
    weights = pl.pallas_call(
        functools.partial(weights_kernel, per_step=per_step, per_dev=per_dev,
                          scaling=HD ** (-0.5)),
        grid_spec=pltpu.PrefetchScalarGridSpec(
            num_scalar_prefetch=3,
            grid=(blocks // per_step,),
            in_specs=[
                pl.BlockSpec((per_src, per_dev * BLK, HD), lambda b, *_: (b, 0, 0)),
                pl.BlockSpec((nk, HD), lambda b, *_: (0, 0)),
            ],
            out_specs=pl.BlockSpec((per_step, BLK, width), lambda b, *_: (b, 0, 0)),
            scratch_shapes=[pltpu.VMEM((width, HD), jnp.bfloat16)],
        ),
        out_shape=jax.ShapeDtypeStruct((blocks, BLK, width), jnp.bfloat16),
        compiler_params=pltpu.CompilerParams(dimension_semantics=("arbitrary",)),
        cost_estimate=pl.CostEstimate(
            flops=blocks * 2 * BLK * width * HD,
            transcendentals=blocks * BLK * width,
            bytes_accessed=k_rows.size * 2 + blocks * BLK * (HD + width) * 2,
        ),
    )(step_size, flat_lists, counts, q_src, k_rows)
    return pl.pallas_call(
        functools.partial(mix_kernel, per_step=per_step),
        grid_spec=pltpu.PrefetchScalarGridSpec(
            num_scalar_prefetch=2,
            grid=(blocks // per_step,),
            in_specs=[
                pl.BlockSpec((per_step, BLK, width), lambda b, *_: (b, 0, 0)),
                pl.BlockSpec((nk, HD), lambda b, *_: (0, 0)),
            ],
            out_specs=pl.BlockSpec((per_step, BLK, HD), lambda b, *_: (b, 0, 0)),
            scratch_shapes=[pltpu.VMEM((width, HD), jnp.bfloat16)],
        ),
        out_shape=jax.ShapeDtypeStruct((blocks, BLK, HD), jnp.bfloat16),
        compiler_params=pltpu.CompilerParams(dimension_semantics=("arbitrary",)),
        cost_estimate=pl.CostEstimate(
            flops=blocks * 2 * BLK * width * HD,
            transcendentals=0,
            bytes_accessed=v_rows.size * 2 + blocks * BLK * (HD + width) * 2,
        ),
    )(step_size, flat_lists, weights, v_rows)


def per_device(queries, keys, values, key_lists, counts, *, x_count):
    group = ("y", "core", "x")
    pb_count = lax.axis_size("y") * lax.axis_size("core")
    z_count = lax.axis_size("z")
    group_count = pb_count * x_count
    kv_count = z_count * x_count
    assert HEADS == group_count
    tokens = keys.shape[0]
    assert BLK == x_count * tokens
    rows = queries.shape[0]
    per_dev = rows // BLK
    meta_width = per_dev * (MOST + 1)
    meta_rows = 16
    assert meta_width <= HD

    kv_heads = jnp.concatenate(
        [
            keys.reshape(tokens, HEADS, HD).transpose(1, 0, 2),
            values.reshape(tokens, HEADS, HD).transpose(1, 0, 2),
        ],
        axis=2,
    )
    kv_split = lax.all_to_all(kv_heads, group, split_axis=0, concat_axis=0, tiled=True)
    kv_part = kv_split.reshape(group_count * tokens, 2 * HD)
    k_rows = lax.all_gather(kv_part[:, :HD], "z", axis=0, tiled=True)
    v_rows = lax.all_gather(kv_part[:, HD:], "z", axis=0, tiled=True)

    kv_index = lax.axis_index("z") * x_count + lax.axis_index("x")
    own_lists = lax.dynamic_slice_in_dim(key_lists, kv_index * per_dev, per_dev, axis=0)
    own_counts = lax.dynamic_slice_in_dim(counts, kv_index * per_dev, per_dev, axis=0)
    meta = jnp.concatenate([own_lists, own_counts[:, None]], axis=1).reshape(-1)
    meta_block = jnp.zeros((meta_rows, HD), jnp.bfloat16).at[0, :meta_width].set(
        meta.astype(jnp.bfloat16)
    )
    q_heads = jnp.concatenate(
        [
            queries.reshape(rows, HEADS, HD).transpose(1, 0, 2),
            jnp.broadcast_to(meta_block[None], (HEADS, meta_rows, HD)),
        ],
        axis=1,
    )
    q_src = lax.all_to_all(q_heads, group, split_axis=0, concat_axis=0, tiled=True)

    meta_in = q_src[:, rows, :meta_width].astype(jnp.int32)
    meta_in = meta_in.reshape(group_count * per_dev, MOST + 1)
    lists = meta_in[:, :MOST]
    lists = (lists % z_count) * pb_count + lists // z_count
    local_counts = meta_in[:, MOST]

    produced = attend(q_src, k_rows, v_rows, lists, local_counts, per_dev)
    back = lax.all_to_all(
        produced.reshape(group_count, rows, HD), group, split_axis=0, concat_axis=0, tiled=True
    )
    return back.transpose(1, 0, 2).reshape(queries.shape)


def solution(mesh):
    pb_count, kv_count = mesh.shape["pb"], mesh.shape["kv"]
    x_count = 4
    fine = jax.sharding.Mesh(
        mesh.devices.reshape(pb_count // 2, 2, kv_count // x_count, x_count),
        ("y", "core", "z", "x"),
    )
    rows = P(("y", "core", "z", "x"), None)
    return jax.shard_map(
        functools.partial(per_device, x_count=x_count),
        mesh=fine,
        in_specs=(rows, rows, rows, P(("y", "core"), None), P(("y", "core"))),
        out_specs=rows,
        check_vma=False,
    )
```

```python
import functools

import jax
import jax.numpy as jnp
from jax import lax
from jax.experimental import pallas as pl
from jax.experimental.pallas import tpu as pltpu
from jax.sharding import PartitionSpec as P

HEADS = 32
HD = 128
BLK = 128
MOST = 8


SLOT_SIZES = (2, 4, MOST)


def weights_kernel(step_ref, lists_ref, counts_ref, q_ref, k_ref, w_ref, kc_ref,
                   *, per_step, per_dev, scaling):
    step = pl.program_id(0)

    def body_for(slots):
        def body():
            for i in range(per_step):
                qb = step * per_step + i
                cnt = counts_ref[qb]
                q = q_ref[i // per_dev, pl.ds((i % per_dev) * BLK, BLK), :]
                for s in range(slots):
                    kb = lists_ref[qb * MOST + s]
                    start = pl.multiple_of(kb * BLK, BLK)
                    kc_ref[pl.ds(s * BLK, BLK), :] = k_ref[pl.ds(start, BLK), :]
                sc = lax.dot_general(q, kc_ref[pl.ds(0, slots * BLK), :], (((1,), (1,)), ((), ())),
                                     preferred_element_type=jnp.float32) * scaling
                slot = lax.broadcasted_iota(jnp.int32, sc.shape, 1) // BLK
                sc = jnp.where(slot < cnt, sc, -jnp.inf)
                m = jnp.max(sc, axis=-1, keepdims=True)
                p = jnp.exp(sc - m)
                l = jnp.sum(p, axis=-1, keepdims=True)
                w_ref[i, :, pl.ds(0, slots * BLK)] = (p / l).astype(jnp.bfloat16)
        return body

    lax.switch(step_ref[step], [body_for(n) for n in SLOT_SIZES])


def mix_kernel(step_ref, lists_ref, w_ref, v_ref, o_ref, vc_ref, *, per_step):
    step = pl.program_id(0)

    def body_for(slots):
        def body():
            for i in range(per_step):
                qb = step * per_step + i
                for s in range(slots):
                    kb = lists_ref[qb * MOST + s]
                    start = pl.multiple_of(kb * BLK, BLK)
                    vc_ref[pl.ds(s * BLK, BLK), :] = v_ref[pl.ds(start, BLK), :]
                w = w_ref[i, :, pl.ds(0, slots * BLK)]
                out = jnp.dot(w, vc_ref[pl.ds(0, slots * BLK), :],
                              preferred_element_type=jnp.float32)
                o_ref[i] = out.astype(o_ref.dtype)
        return body

    lax.switch(step_ref[step], [body_for(n) for n in SLOT_SIZES])


def attend(q_src, kv_rows, lists, counts, per_dev):
    sources = q_src.shape[0]
    blocks = sources * per_dev
    per_src = 4 if sources % 4 == 0 else 1
    per_step = per_src * per_dev
    nk = kv_rows.shape[0]
    width = MOST * BLK
    widest = jnp.max(counts.reshape(blocks // per_step, per_step), axis=1)
    step_size = jnp.zeros_like(widest)
    for n in SLOT_SIZES[:-1]:
        step_size = step_size + (widest > n).astype(jnp.int32)
    flat_lists = lists.reshape(-1)
    weights = pl.pallas_call(
        functools.partial(weights_kernel, per_step=per_step, per_dev=per_dev,
                          scaling=HD ** (-0.5)),
        grid_spec=pltpu.PrefetchScalarGridSpec(
            num_scalar_prefetch=3,
            grid=(blocks // per_step,),
            in_specs=[
                pl.BlockSpec((per_src, per_dev * BLK, HD), lambda b, *_: (b, 0, 0)),
                pl.BlockSpec((nk, HD), lambda b, *_: (0, 0)),
            ],
            out_specs=pl.BlockSpec((per_step, BLK, width), lambda b, *_: (b, 0, 0)),
            scratch_shapes=[pltpu.VMEM((width, HD), jnp.bfloat16)],
        ),
        out_shape=jax.ShapeDtypeStruct((blocks, BLK, width), jnp.bfloat16),
        compiler_params=pltpu.CompilerParams(dimension_semantics=("arbitrary",)),
        cost_estimate=pl.CostEstimate(
            flops=blocks * 2 * BLK * width * HD,
            transcendentals=blocks * BLK * width,
            bytes_accessed=kv_rows.size + blocks * BLK * (HD + width) * 2,
        ),
    )(step_size, flat_lists, counts, q_src, kv_rows)
    return pl.pallas_call(
        functools.partial(mix_kernel, per_step=per_step),
        grid_spec=pltpu.PrefetchScalarGridSpec(
            num_scalar_prefetch=2,
            grid=(blocks // per_step,),
            in_specs=[
                pl.BlockSpec((per_step, BLK, width), lambda b, *_: (b, 0, 0)),
                pl.BlockSpec((nk, HD), lambda b, *_: (0, 1)),
            ],
            out_specs=pl.BlockSpec((per_step, BLK, HD), lambda b, *_: (b, 0, 0)),
            scratch_shapes=[pltpu.VMEM((width, HD), jnp.bfloat16)],
        ),
        out_shape=jax.ShapeDtypeStruct((blocks, BLK, HD), jnp.bfloat16),
        compiler_params=pltpu.CompilerParams(dimension_semantics=("arbitrary",)),
        cost_estimate=pl.CostEstimate(
            flops=blocks * 2 * BLK * width * HD,
            transcendentals=0,
            bytes_accessed=kv_rows.size + blocks * BLK * (HD + width) * 2,
        ),
    )(step_size, flat_lists, weights, kv_rows)


def per_device(queries, keys, values, key_lists, counts, *, x_count):
    group = ("y", "core", "x")
    pb_count = lax.axis_size("y") * lax.axis_size("core")
    z_count = lax.axis_size("z")
    group_count = pb_count * x_count
    kv_count = z_count * x_count
    assert HEADS == group_count
    tokens = keys.shape[0]
    assert BLK == x_count * tokens
    rows = queries.shape[0]
    per_dev = rows // BLK
    meta_width = per_dev * (MOST + 1)
    meta_rows = 16
    assert meta_width <= HD

    kv_heads = jnp.concatenate(
        [
            keys.reshape(tokens, HEADS, HD).transpose(1, 0, 2),
            values.reshape(tokens, HEADS, HD).transpose(1, 0, 2),
        ],
        axis=2,
    )
    kv_split = lax.all_to_all(kv_heads, group, split_axis=0, concat_axis=0, tiled=True)
    kv_part = kv_split.reshape(group_count * tokens, 2 * HD)
    kv_rows = lax.all_gather(kv_part, "z", axis=0, tiled=True)

    kv_index = lax.axis_index("z") * x_count + lax.axis_index("x")
    own_lists = lax.dynamic_slice_in_dim(key_lists, kv_index * per_dev, per_dev, axis=0)
    own_counts = lax.dynamic_slice_in_dim(counts, kv_index * per_dev, per_dev, axis=0)
    meta = jnp.concatenate([own_lists, own_counts[:, None]], axis=1).reshape(-1)
    meta_block = jnp.zeros((meta_rows, HD), jnp.bfloat16).at[0, :meta_width].set(
        meta.astype(jnp.bfloat16)
    )
    q_heads = jnp.concatenate(
        [
            queries.reshape(rows, HEADS, HD).transpose(1, 0, 2),
            jnp.broadcast_to(meta_block[None], (HEADS, meta_rows, HD)),
        ],
        axis=1,
    )
    q_src = lax.all_to_all(q_heads, group, split_axis=0, concat_axis=0, tiled=True)

    meta_in = q_src[:, rows, :meta_width].astype(jnp.int32)
    meta_in = meta_in.reshape(group_count * per_dev, MOST + 1)
    lists = meta_in[:, :MOST]
    lists = (lists % z_count) * pb_count + lists // z_count
    local_counts = meta_in[:, MOST]

    produced = attend(q_src, kv_rows, lists, local_counts, per_dev)
    back = lax.all_to_all(
        produced.reshape(group_count, rows, HD), group, split_axis=0, concat_axis=0, tiled=True
    )
    return back.transpose(1, 0, 2).reshape(queries.shape)


def solution(mesh):
    pb_count, kv_count = mesh.shape["pb"], mesh.shape["kv"]
    x_count = 4
    fine = jax.sharding.Mesh(
        mesh.devices.reshape(pb_count // 2, 2, kv_count // x_count, x_count),
        ("y", "core", "z", "x"),
    )
    rows = P(("y", "core", "z", "x"), None)
    return jax.shard_map(
        functools.partial(per_device, x_count=x_count),
        mesh=fine,
        in_specs=(rows, rows, rows, P(("y", "core"), None), P(("y", "core"))),
        out_specs=rows,
        check_vma=False,
    )
```

```python
import functools

import jax
import jax.numpy as jnp
from jax import lax
from jax.experimental import pallas as pl
from jax.experimental.pallas import tpu as pltpu
from jax.sharding import PartitionSpec as P

HEADS = 32
HD = 128
BLK = 128
MOST = 8


SLOT_SIZES = (2, 4, 6, MOST)


def weights_kernel(step_ref, lists_ref, counts_ref, q_ref, k_ref, w_ref, kc_ref,
                   *, per_step, per_dev, scaling):
    step = pl.program_id(0)

    def body_for(slots):
        def body():
            for i in range(per_step):
                qb = step * per_step + i
                cnt = counts_ref[qb]
                q = q_ref[i // per_dev, pl.ds((i % per_dev) * BLK, BLK), :]
                for s in range(slots):
                    kb = lists_ref[qb * MOST + s]
                    start = pl.multiple_of(kb * BLK, BLK)
                    kc_ref[pl.ds(s * BLK, BLK), :] = k_ref[pl.ds(start, BLK), :]
                sc = lax.dot_general(q, kc_ref[pl.ds(0, slots * BLK), :], (((1,), (1,)), ((), ())),
                                     preferred_element_type=jnp.float32) * scaling
                slot = lax.broadcasted_iota(jnp.int32, sc.shape, 1) // BLK
                sc = jnp.where(slot < cnt, sc, -jnp.inf)
                m = jnp.max(sc, axis=-1, keepdims=True)
                p = jnp.exp(sc - m)
                l = jnp.sum(p, axis=-1, keepdims=True)
                w_ref[i, :, pl.ds(0, slots * BLK)] = (p / l).astype(jnp.bfloat16)
        return body

    lax.switch(step_ref[step], [body_for(n) for n in SLOT_SIZES])


def mix_kernel(step_ref, lists_ref, w_ref, v_ref, o_ref, vc_ref, *, per_step):
    step = pl.program_id(0)

    def body_for(slots):
        def body():
            for i in range(per_step):
                qb = step * per_step + i
                for s in range(slots):
                    kb = lists_ref[qb * MOST + s]
                    start = pl.multiple_of(kb * BLK, BLK)
                    vc_ref[pl.ds(s * BLK, BLK), :] = v_ref[pl.ds(start, BLK), :]
                w = w_ref[i, :, pl.ds(0, slots * BLK)]
                out = jnp.dot(w, vc_ref[pl.ds(0, slots * BLK), :],
                              preferred_element_type=jnp.float32)
                o_ref[i] = out.astype(o_ref.dtype)
        return body

    lax.switch(step_ref[step], [body_for(n) for n in SLOT_SIZES])


def attend(q_src, kv_rows, lists, counts, per_dev):
    sources = q_src.shape[0]
    blocks = sources * per_dev
    per_src = 4 if sources % 4 == 0 else 1
    per_step = per_src * per_dev
    nk = kv_rows.shape[0]
    width = MOST * BLK
    widest = jnp.max(counts.reshape(blocks // per_step, per_step), axis=1)
    step_size = jnp.zeros_like(widest)
    for n in SLOT_SIZES[:-1]:
        step_size = step_size + (widest > n).astype(jnp.int32)
    flat_lists = lists.reshape(-1)
    weights = pl.pallas_call(
        functools.partial(weights_kernel, per_step=per_step, per_dev=per_dev,
                          scaling=HD ** (-0.5)),
        grid_spec=pltpu.PrefetchScalarGridSpec(
            num_scalar_prefetch=3,
            grid=(blocks // per_step,),
            in_specs=[
                pl.BlockSpec((per_src, per_dev * BLK, HD), lambda b, *_: (b, 0, 0)),
                pl.BlockSpec((nk, HD), lambda b, *_: (0, 0)),
            ],
            out_specs=pl.BlockSpec((per_step, BLK, width), lambda b, *_: (b, 0, 0)),
            scratch_shapes=[pltpu.VMEM((width, HD), jnp.bfloat16)],
        ),
        out_shape=jax.ShapeDtypeStruct((blocks, BLK, width), jnp.bfloat16),
        compiler_params=pltpu.CompilerParams(dimension_semantics=("arbitrary",)),
        cost_estimate=pl.CostEstimate(
            flops=blocks * 2 * BLK * width * HD,
            transcendentals=blocks * BLK * width,
            bytes_accessed=kv_rows.size + blocks * BLK * (HD + width) * 2,
        ),
    )(step_size, flat_lists, counts, q_src, kv_rows)
    return pl.pallas_call(
        functools.partial(mix_kernel, per_step=per_step),
        grid_spec=pltpu.PrefetchScalarGridSpec(
            num_scalar_prefetch=2,
            grid=(blocks // per_step,),
            in_specs=[
                pl.BlockSpec((per_step, BLK, width), lambda b, *_: (b, 0, 0)),
                pl.BlockSpec((nk, HD), lambda b, *_: (0, 1)),
            ],
            out_specs=pl.BlockSpec((per_step, BLK, HD), lambda b, *_: (b, 0, 0)),
            scratch_shapes=[pltpu.VMEM((width, HD), jnp.bfloat16)],
        ),
        out_shape=jax.ShapeDtypeStruct((blocks, BLK, HD), jnp.bfloat16),
        compiler_params=pltpu.CompilerParams(dimension_semantics=("arbitrary",)),
        cost_estimate=pl.CostEstimate(
            flops=blocks * 2 * BLK * width * HD,
            transcendentals=0,
            bytes_accessed=kv_rows.size + blocks * BLK * (HD + width) * 2,
        ),
    )(step_size, flat_lists, weights, kv_rows)


def per_device(queries, keys, values, key_lists, counts, *, x_count):
    group = ("y", "core", "x")
    pb_count = lax.axis_size("y") * lax.axis_size("core")
    z_count = lax.axis_size("z")
    group_count = pb_count * x_count
    kv_count = z_count * x_count
    assert HEADS == group_count
    tokens = keys.shape[0]
    assert BLK == x_count * tokens
    rows = queries.shape[0]
    per_dev = rows // BLK
    meta_width = per_dev * (MOST + 1)
    meta_rows = 16
    assert meta_width <= HD

    kv_heads = jnp.concatenate(
        [
            keys.reshape(tokens, HEADS, HD).transpose(1, 0, 2),
            values.reshape(tokens, HEADS, HD).transpose(1, 0, 2),
        ],
        axis=2,
    )
    kv_split = lax.all_to_all(kv_heads, group, split_axis=0, concat_axis=0, tiled=True)
    kv_part = kv_split.reshape(group_count * tokens, 2 * HD)
    kv_rows = lax.all_gather(kv_part, "z", axis=0, tiled=True)

    kv_index = lax.axis_index("z") * x_count + lax.axis_index("x")
    own_lists = lax.dynamic_slice_in_dim(key_lists, kv_index * per_dev, per_dev, axis=0)
    own_counts = lax.dynamic_slice_in_dim(counts, kv_index * per_dev, per_dev, axis=0)
    meta = jnp.concatenate([own_lists, own_counts[:, None]], axis=1).reshape(-1)
    meta_block = jnp.zeros((meta_rows, HD), jnp.bfloat16).at[0, :meta_width].set(
        meta.astype(jnp.bfloat16)
    )
    q_heads = jnp.concatenate(
        [
            queries.reshape(rows, HEADS, HD).transpose(1, 0, 2),
            jnp.broadcast_to(meta_block[None], (HEADS, meta_rows, HD)),
        ],
        axis=1,
    )
    q_src = lax.all_to_all(q_heads, group, split_axis=0, concat_axis=0, tiled=True)

    meta_in = q_src[:, rows, :meta_width].astype(jnp.int32)
    meta_in = meta_in.reshape(group_count * per_dev, MOST + 1)
    lists = meta_in[:, :MOST]
    lists = (lists % z_count) * pb_count + lists // z_count
    local_counts = meta_in[:, MOST]

    produced = attend(q_src, kv_rows, lists, local_counts, per_dev)
    back = lax.all_to_all(
        produced.reshape(group_count, rows, HD), group, split_axis=0, concat_axis=0, tiled=True
    )
    return back.transpose(1, 0, 2).reshape(queries.shape)


def solution(mesh):
    pb_count, kv_count = mesh.shape["pb"], mesh.shape["kv"]
    x_count = 4
    fine = jax.sharding.Mesh(
        mesh.devices.reshape(pb_count // 2, 2, kv_count // x_count, x_count),
        ("y", "core", "z", "x"),
    )
    rows = P(("y", "core", "z", "x"), None)
    return jax.shard_map(
        functools.partial(per_device, x_count=x_count),
        mesh=fine,
        in_specs=(rows, rows, rows, P(("y", "core"), None), P(("y", "core"))),
        out_specs=rows,
        check_vma=False,
    )
```

```python
import functools

import jax
import jax.numpy as jnp
from jax import lax
from jax.experimental import pallas as pl
from jax.experimental.pallas import tpu as pltpu
from jax.sharding import PartitionSpec as P

HEADS = 32
HD = 128
BLK = 128
MOST = 8


SLOT_SIZES = (2, 3, 4, 5, 6, 7, MOST)


def weights_kernel(step_ref, lists_ref, counts_ref, q_ref, k_ref, w_ref, kc_ref,
                   *, per_step, per_dev, scaling):
    step = pl.program_id(0)

    def body_for(slots):
        def body():
            for i in range(per_step):
                qb = step * per_step + i
                cnt = counts_ref[qb]
                q = q_ref[i // per_dev, pl.ds((i % per_dev) * BLK, BLK), :]
                for s in range(slots):
                    kb = lists_ref[qb * MOST + s]
                    start = pl.multiple_of(kb * BLK, BLK)
                    kc_ref[pl.ds(s * BLK, BLK), :] = k_ref[pl.ds(start, BLK), :]
                sc = lax.dot_general(q, kc_ref[pl.ds(0, slots * BLK), :], (((1,), (1,)), ((), ())),
                                     preferred_element_type=jnp.float32) * scaling
                slot = lax.broadcasted_iota(jnp.int32, sc.shape, 1) // BLK
                sc = jnp.where(slot < cnt, sc, -jnp.inf)
                m = jnp.max(sc, axis=-1, keepdims=True)
                p = jnp.exp(sc - m)
                l = jnp.sum(p, axis=-1, keepdims=True)
                w_ref[i, :, pl.ds(0, slots * BLK)] = (p / l).astype(jnp.bfloat16)
        return body

    lax.switch(step_ref[step], [body_for(n) for n in SLOT_SIZES])


def mix_kernel(step_ref, lists_ref, w_ref, v_ref, o_ref, vc_ref, *, per_step):
    step = pl.program_id(0)

    def body_for(slots):
        def body():
            for i in range(per_step):
                qb = step * per_step + i
                for s in range(slots):
                    kb = lists_ref[qb * MOST + s]
                    start = pl.multiple_of(kb * BLK, BLK)
                    vc_ref[pl.ds(s * BLK, BLK), :] = v_ref[pl.ds(start, BLK), :]
                w = w_ref[i, :, pl.ds(0, slots * BLK)]
                out = jnp.dot(w, vc_ref[pl.ds(0, slots * BLK), :],
                              preferred_element_type=jnp.float32)
                o_ref[i] = out.astype(o_ref.dtype)
        return body

    lax.switch(step_ref[step], [body_for(n) for n in SLOT_SIZES])


def attend(q_src, kv_rows, lists, counts, per_dev):
    sources = q_src.shape[0]
    blocks = sources * per_dev
    per_src = 4 if sources % 4 == 0 else 1
    per_step = per_src * per_dev
    nk = kv_rows.shape[0]
    width = MOST * BLK
    widest = jnp.max(counts.reshape(blocks // per_step, per_step), axis=1)
    step_size = jnp.zeros_like(widest)
    for n in SLOT_SIZES[:-1]:
        step_size = step_size + (widest > n).astype(jnp.int32)
    flat_lists = lists.reshape(-1)
    weights = pl.pallas_call(
        functools.partial(weights_kernel, per_step=per_step, per_dev=per_dev,
                          scaling=HD ** (-0.5)),
        grid_spec=pltpu.PrefetchScalarGridSpec(
            num_scalar_prefetch=3,
            grid=(blocks // per_step,),
            in_specs=[
                pl.BlockSpec((per_src, per_dev * BLK, HD), lambda b, *_: (b, 0, 0)),
                pl.BlockSpec((nk, HD), lambda b, *_: (0, 0)),
            ],
            out_specs=pl.BlockSpec((per_step, BLK, width), lambda b, *_: (b, 0, 0)),
            scratch_shapes=[pltpu.VMEM((width, HD), jnp.bfloat16)],
        ),
        out_shape=jax.ShapeDtypeStruct((blocks, BLK, width), jnp.bfloat16),
        compiler_params=pltpu.CompilerParams(dimension_semantics=("arbitrary",)),
        cost_estimate=pl.CostEstimate(
            flops=blocks * 2 * BLK * width * HD,
            transcendentals=blocks * BLK * width,
            bytes_accessed=kv_rows.size + blocks * BLK * (HD + width) * 2,
        ),
    )(step_size, flat_lists, counts, q_src, kv_rows)
    return pl.pallas_call(
        functools.partial(mix_kernel, per_step=per_step),
        grid_spec=pltpu.PrefetchScalarGridSpec(
            num_scalar_prefetch=2,
            grid=(blocks // per_step,),
            in_specs=[
                pl.BlockSpec((per_step, BLK, width), lambda b, *_: (b, 0, 0)),
                pl.BlockSpec((nk, HD), lambda b, *_: (0, 1)),
            ],
            out_specs=pl.BlockSpec((per_step, BLK, HD), lambda b, *_: (b, 0, 0)),
            scratch_shapes=[pltpu.VMEM((width, HD), jnp.bfloat16)],
        ),
        out_shape=jax.ShapeDtypeStruct((blocks, BLK, HD), jnp.bfloat16),
        compiler_params=pltpu.CompilerParams(dimension_semantics=("arbitrary",)),
        cost_estimate=pl.CostEstimate(
            flops=blocks * 2 * BLK * width * HD,
            transcendentals=0,
            bytes_accessed=kv_rows.size + blocks * BLK * (HD + width) * 2,
        ),
    )(step_size, flat_lists, weights, kv_rows)


def per_device(queries, keys, values, key_lists, counts, *, x_count):
    group = ("y", "core", "x")
    pb_count = lax.axis_size("y") * lax.axis_size("core")
    z_count = lax.axis_size("z")
    group_count = pb_count * x_count
    kv_count = z_count * x_count
    assert HEADS == group_count
    tokens = keys.shape[0]
    assert BLK == x_count * tokens
    rows = queries.shape[0]
    per_dev = rows // BLK
    meta_width = per_dev * (MOST + 1)
    meta_rows = 16
    assert meta_width <= HD

    kv_heads = jnp.concatenate(
        [
            keys.reshape(tokens, HEADS, HD).transpose(1, 0, 2),
            values.reshape(tokens, HEADS, HD).transpose(1, 0, 2),
        ],
        axis=2,
    )
    kv_split = lax.all_to_all(kv_heads, group, split_axis=0, concat_axis=0, tiled=True)
    kv_part = kv_split.reshape(group_count * tokens, 2 * HD)
    kv_rows = lax.all_gather(kv_part, "z", axis=0, tiled=True)

    kv_index = lax.axis_index("z") * x_count + lax.axis_index("x")
    own_lists = lax.dynamic_slice_in_dim(key_lists, kv_index * per_dev, per_dev, axis=0)
    own_counts = lax.dynamic_slice_in_dim(counts, kv_index * per_dev, per_dev, axis=0)
    meta = jnp.concatenate([own_lists, own_counts[:, None]], axis=1).reshape(-1)
    meta_block = jnp.zeros((meta_rows, HD), jnp.bfloat16).at[0, :meta_width].set(
        meta.astype(jnp.bfloat16)
    )
    q_heads = jnp.concatenate(
        [
            queries.reshape(rows, HEADS, HD).transpose(1, 0, 2),
            jnp.broadcast_to(meta_block[None], (HEADS, meta_rows, HD)),
        ],
        axis=1,
    )
    q_src = lax.all_to_all(q_heads, group, split_axis=0, concat_axis=0, tiled=True)

    meta_in = q_src[:, rows, :meta_width].astype(jnp.int32)
    meta_in = meta_in.reshape(group_count * per_dev, MOST + 1)
    lists = meta_in[:, :MOST]
    lists = (lists % z_count) * pb_count + lists // z_count
    local_counts = meta_in[:, MOST]

    produced = attend(q_src, kv_rows, lists, local_counts, per_dev)
    back = lax.all_to_all(
        produced.reshape(group_count, rows, HD), group, split_axis=0, concat_axis=0, tiled=True
    )
    return back.transpose(1, 0, 2).reshape(queries.shape)


def solution(mesh):
    pb_count, kv_count = mesh.shape["pb"], mesh.shape["kv"]
    x_count = 4
    fine = jax.sharding.Mesh(
        mesh.devices.reshape(pb_count // 2, 2, kv_count // x_count, x_count),
        ("y", "core", "z", "x"),
    )
    rows = P(("y", "core", "z", "x"), None)
    return jax.shard_map(
        functools.partial(per_device, x_count=x_count),
        mesh=fine,
        in_specs=(rows, rows, rows, P(("y", "core"), None), P(("y", "core"))),
        out_specs=rows,
        check_vma=False,
    )
```

```python
import functools

import jax
import jax.numpy as jnp
from jax import lax
from jax.experimental import pallas as pl
from jax.experimental.pallas import tpu as pltpu
from jax.sharding import PartitionSpec as P

HEADS = 32
HD = 128
BLK = 128
MOST = 8


SLOT_SIZES = (2, 3, 4, 5, 6, 7, MOST)
HALF = MOST // 2


def weights_kernel(step_ref, hi_ref, lists_ref, counts_ref, q_ref, k_ref, wlo_ref, whi_ref, kc_ref,
                   *, per_step, per_dev, scaling):
    step = pl.program_id(0)

    def body_for(slots):
        def body():
            for i in range(per_step):
                qb = step * per_step + i
                cnt = counts_ref[qb]
                q = q_ref[i // per_dev, pl.ds((i % per_dev) * BLK, BLK), :]
                for s in range(slots):
                    kb = lists_ref[qb * MOST + s]
                    start = pl.multiple_of(kb * BLK, BLK)
                    kc_ref[pl.ds(s * BLK, BLK), :] = k_ref[pl.ds(start, BLK), :]
                sc = lax.dot_general(q, kc_ref[pl.ds(0, slots * BLK), :], (((1,), (1,)), ((), ())),
                                     preferred_element_type=jnp.float32) * scaling
                slot = lax.broadcasted_iota(jnp.int32, sc.shape, 1) // BLK
                sc = jnp.where(slot < cnt, sc, -jnp.inf)
                m = jnp.max(sc, axis=-1, keepdims=True)
                p = jnp.exp(sc - m)
                l = jnp.sum(p, axis=-1, keepdims=True)
                w = (p / l).astype(jnp.bfloat16)
                low = min(slots, HALF) * BLK
                wlo_ref[i, :, pl.ds(0, low)] = w[:, :low]
                if slots > HALF:
                    whi_ref[i, :, pl.ds(0, slots * BLK - low)] = w[:, low:]
        return body

    lax.switch(step_ref[step], [body_for(n) for n in SLOT_SIZES])


def mix_kernel(step_ref, hi_ref, lists_ref, wlo_ref, whi_ref, v_ref, o_ref, vc_ref, *, per_step):
    step = pl.program_id(0)

    def body_for(slots):
        def body():
            for i in range(per_step):
                qb = step * per_step + i
                for s in range(slots):
                    kb = lists_ref[qb * MOST + s]
                    start = pl.multiple_of(kb * BLK, BLK)
                    vc_ref[pl.ds(s * BLK, BLK), :] = v_ref[pl.ds(start, BLK), :]
                low = min(slots, HALF) * BLK
                out = jnp.dot(wlo_ref[i, :, pl.ds(0, low)], vc_ref[pl.ds(0, low), :],
                              preferred_element_type=jnp.float32)
                if slots > HALF:
                    out = out + jnp.dot(whi_ref[i, :, pl.ds(0, slots * BLK - low)],
                                        vc_ref[pl.ds(low, slots * BLK - low), :],
                                        preferred_element_type=jnp.float32)
                o_ref[i] = out.astype(o_ref.dtype)
        return body

    lax.switch(step_ref[step], [body_for(n) for n in SLOT_SIZES])


def attend(q_src, kv_rows, lists, counts, per_dev):
    sources = q_src.shape[0]
    blocks = sources * per_dev
    per_src = 4 if sources % 4 == 0 else 1
    per_step = per_src * per_dev
    nk = kv_rows.shape[0]
    width = HALF * BLK
    widest = jnp.max(counts.reshape(blocks // per_step, per_step), axis=1)
    step_size = jnp.zeros_like(widest)
    for n in SLOT_SIZES[:-1]:
        step_size = step_size + (widest > n).astype(jnp.int32)
    flat_lists = lists.reshape(-1)
    steps = blocks // per_step
    big = widest > HALF
    hi_index = lax.cummax(jnp.where(big, jnp.arange(steps, dtype=jnp.int32), 0))
    weights = pl.pallas_call(
        functools.partial(weights_kernel, per_step=per_step, per_dev=per_dev,
                          scaling=HD ** (-0.5)),
        grid_spec=pltpu.PrefetchScalarGridSpec(
            num_scalar_prefetch=4,
            grid=(blocks // per_step,),
            in_specs=[
                pl.BlockSpec((per_src, per_dev * BLK, HD), lambda b, *_: (b, 0, 0)),
                pl.BlockSpec((nk, HD), lambda b, *_: (0, 0)),
            ],
            out_specs=[
                pl.BlockSpec((per_step, BLK, width), lambda b, *_: (b, 0, 0)),
                pl.BlockSpec((per_step, BLK, width), lambda b, s, h, *_: (h[b], 0, 0)),
            ],
            scratch_shapes=[pltpu.VMEM((MOST * BLK, HD), jnp.bfloat16)],
        ),
        out_shape=[jax.ShapeDtypeStruct((blocks, BLK, width), jnp.bfloat16)] * 2,
        compiler_params=pltpu.CompilerParams(dimension_semantics=("arbitrary",)),
        cost_estimate=pl.CostEstimate(
            flops=blocks * 2 * BLK * width * HD,
            transcendentals=blocks * BLK * width,
            bytes_accessed=kv_rows.size + blocks * BLK * (HD + width) * 2,
        ),
    )(step_size, hi_index, flat_lists, counts, q_src, kv_rows)
    return pl.pallas_call(
        functools.partial(mix_kernel, per_step=per_step),
        grid_spec=pltpu.PrefetchScalarGridSpec(
            num_scalar_prefetch=3,
            grid=(blocks // per_step,),
            in_specs=[
                pl.BlockSpec((per_step, BLK, width), lambda b, *_: (b, 0, 0)),
                pl.BlockSpec((per_step, BLK, width), lambda b, s, h, *_: (h[b], 0, 0)),
                pl.BlockSpec((nk, HD), lambda b, *_: (0, 1)),
            ],
            out_specs=pl.BlockSpec((per_step, BLK, HD), lambda b, *_: (b, 0, 0)),
            scratch_shapes=[pltpu.VMEM((MOST * BLK, HD), jnp.bfloat16)],
        ),
        out_shape=jax.ShapeDtypeStruct((blocks, BLK, HD), jnp.bfloat16),
        compiler_params=pltpu.CompilerParams(dimension_semantics=("arbitrary",)),
        cost_estimate=pl.CostEstimate(
            flops=blocks * 2 * BLK * width * HD,
            transcendentals=0,
            bytes_accessed=kv_rows.size + blocks * BLK * (HD + width) * 2,
        ),
    )(step_size, hi_index, flat_lists, weights[0], weights[1], kv_rows)


def per_device(queries, keys, values, key_lists, counts, *, x_count):
    group = ("y", "core", "x")
    pb_count = lax.axis_size("y") * lax.axis_size("core")
    z_count = lax.axis_size("z")
    group_count = pb_count * x_count
    kv_count = z_count * x_count
    assert HEADS == group_count
    tokens = keys.shape[0]
    assert BLK == x_count * tokens
    rows = queries.shape[0]
    per_dev = rows // BLK
    meta_width = per_dev * (MOST + 1)
    meta_rows = 16
    assert meta_width <= HD

    kv_heads = jnp.concatenate(
        [
            keys.reshape(tokens, HEADS, HD).transpose(1, 0, 2),
            values.reshape(tokens, HEADS, HD).transpose(1, 0, 2),
        ],
        axis=2,
    )
    kv_split = lax.all_to_all(kv_heads, group, split_axis=0, concat_axis=0, tiled=True)
    kv_part = kv_split.reshape(group_count * tokens, 2 * HD)
    kv_rows = lax.all_gather(kv_part, "z", axis=0, tiled=True)

    kv_index = lax.axis_index("z") * x_count + lax.axis_index("x")
    own_lists = lax.dynamic_slice_in_dim(key_lists, kv_index * per_dev, per_dev, axis=0)
    own_counts = lax.dynamic_slice_in_dim(counts, kv_index * per_dev, per_dev, axis=0)
    meta = jnp.concatenate([own_lists, own_counts[:, None]], axis=1).reshape(-1)
    meta_block = jnp.zeros((meta_rows, HD), jnp.bfloat16).at[0, :meta_width].set(
        meta.astype(jnp.bfloat16)
    )
    q_heads = jnp.concatenate(
        [
            queries.reshape(rows, HEADS, HD).transpose(1, 0, 2),
            jnp.broadcast_to(meta_block[None], (HEADS, meta_rows, HD)),
        ],
        axis=1,
    )
    q_src = lax.all_to_all(q_heads, group, split_axis=0, concat_axis=0, tiled=True)

    meta_in = q_src[:, rows, :meta_width].astype(jnp.int32)
    meta_in = meta_in.reshape(group_count * per_dev, MOST + 1)
    lists = meta_in[:, :MOST]
    lists = (lists % z_count) * pb_count + lists // z_count
    local_counts = meta_in[:, MOST]

    produced = attend(q_src, kv_rows, lists, local_counts, per_dev)
    back = lax.all_to_all(
        produced.reshape(group_count, rows, HD), group, split_axis=0, concat_axis=0, tiled=True
    )
    return back.transpose(1, 0, 2).reshape(queries.shape)


def solution(mesh):
    pb_count, kv_count = mesh.shape["pb"], mesh.shape["kv"]
    x_count = 4
    fine = jax.sharding.Mesh(
        mesh.devices.reshape(pb_count // 2, 2, kv_count // x_count, x_count),
        ("y", "core", "z", "x"),
    )
    rows = P(("y", "core", "z", "x"), None)
    return jax.shard_map(
        functools.partial(per_device, x_count=x_count),
        mesh=fine,
        in_specs=(rows, rows, rows, P(("y", "core"), None), P(("y", "core"))),
        out_specs=rows,
        check_vma=False,
    )
```

```python
import functools

import jax
import jax.numpy as jnp
from jax import lax
from jax.experimental import pallas as pl
from jax.experimental.pallas import tpu as pltpu
from jax.sharding import PartitionSpec as P

HEADS = 32
HD = 128
BLK = 128
MOST = 8


SLOT_SIZES = (2, 3, 4, 5, 6, 7, MOST)


def weights_kernel(step_ref, lists_ref, counts_ref, q_ref, k_ref, w_ref, kc_ref,
                   *, per_step, per_dev, scaling):
    step = pl.program_id(0)

    def body_for(slots):
        def body():
            for i in range(per_step):
                qb = step * per_step + i
                cnt = counts_ref[qb]
                q = q_ref[i // per_dev, pl.ds((i % per_dev) * BLK, BLK), :]
                for s in range(slots):
                    kb = lists_ref[qb * MOST + s]
                    start = pl.multiple_of(kb * BLK, BLK)
                    kc_ref[pl.ds(s * BLK, BLK), :] = k_ref[pl.ds(start, BLK), :]
                sc = lax.dot_general(q, kc_ref[pl.ds(0, slots * BLK), :], (((1,), (1,)), ((), ())),
                                     preferred_element_type=jnp.float32) * scaling
                slot = lax.broadcasted_iota(jnp.int32, sc.shape, 1) // BLK
                sc = jnp.where(slot < cnt, sc, -jnp.inf)
                m = jnp.max(sc, axis=-1, keepdims=True)
                p = jnp.exp(sc - m)
                l = jnp.sum(p, axis=-1, keepdims=True)
                w_ref[i, :, pl.ds(0, slots * BLK)] = (p / l).astype(jnp.bfloat16)
        return body

    lax.switch(step_ref[step], [body_for(n) for n in SLOT_SIZES])


def mix_kernel(step_ref, lists_ref, w_ref, v_ref, o_ref, vc_ref, *, per_step):
    step = pl.program_id(0)

    def body_for(slots):
        def body():
            for i in range(per_step):
                qb = step * per_step + i
                for s in range(slots):
                    kb = lists_ref[qb * MOST + s]
                    start = pl.multiple_of(kb * BLK, BLK)
                    vc_ref[pl.ds(s * BLK, BLK), :] = v_ref[pl.ds(start, BLK), :]
                w = w_ref[i, :, pl.ds(0, slots * BLK)]
                out = jnp.dot(w, vc_ref[pl.ds(0, slots * BLK), :],
                              preferred_element_type=jnp.float32)
                o_ref[i] = out.astype(o_ref.dtype)
        return body

    lax.switch(step_ref[step], [body_for(n) for n in SLOT_SIZES])


def attend(q_src, kv_rows, lists, counts, per_dev):
    sources = q_src.shape[0]
    blocks = sources * per_dev
    per_src = 2 if sources % 2 == 0 else 1
    per_step = per_src * per_dev
    nk = kv_rows.shape[0]
    width = MOST * BLK
    widest = jnp.max(counts.reshape(blocks // per_step, per_step), axis=1)
    step_size = jnp.zeros_like(widest)
    for n in SLOT_SIZES[:-1]:
        step_size = step_size + (widest > n).astype(jnp.int32)
    flat_lists = lists.reshape(-1)
    weights = pl.pallas_call(
        functools.partial(weights_kernel, per_step=per_step, per_dev=per_dev,
                          scaling=HD ** (-0.5)),
        grid_spec=pltpu.PrefetchScalarGridSpec(
            num_scalar_prefetch=3,
            grid=(blocks // per_step,),
            in_specs=[
                pl.BlockSpec((per_src, per_dev * BLK, HD), lambda b, *_: (b, 0, 0)),
                pl.BlockSpec((nk, HD), lambda b, *_: (0, 0)),
            ],
            out_specs=pl.BlockSpec((per_step, BLK, width), lambda b, *_: (b, 0, 0)),
            scratch_shapes=[pltpu.VMEM((width, HD), jnp.bfloat16)],
        ),
        out_shape=jax.ShapeDtypeStruct((blocks, BLK, width), jnp.bfloat16),
        compiler_params=pltpu.CompilerParams(dimension_semantics=("arbitrary",)),
        cost_estimate=pl.CostEstimate(
            flops=blocks * 2 * BLK * width * HD,
            transcendentals=blocks * BLK * width,
            bytes_accessed=kv_rows.size + blocks * BLK * (HD + width) * 2,
        ),
    )(step_size, flat_lists, counts, q_src, kv_rows)
    return pl.pallas_call(
        functools.partial(mix_kernel, per_step=per_step),
        grid_spec=pltpu.PrefetchScalarGridSpec(
            num_scalar_prefetch=2,
            grid=(blocks // per_step,),
            in_specs=[
                pl.BlockSpec((per_step, BLK, width), lambda b, *_: (b, 0, 0)),
                pl.BlockSpec((nk, HD), lambda b, *_: (0, 1)),
            ],
            out_specs=pl.BlockSpec((per_step, BLK, HD), lambda b, *_: (b, 0, 0)),
            scratch_shapes=[pltpu.VMEM((width, HD), jnp.bfloat16)],
        ),
        out_shape=jax.ShapeDtypeStruct((blocks, BLK, HD), jnp.bfloat16),
        compiler_params=pltpu.CompilerParams(dimension_semantics=("arbitrary",)),
        cost_estimate=pl.CostEstimate(
            flops=blocks * 2 * BLK * width * HD,
            transcendentals=0,
            bytes_accessed=kv_rows.size + blocks * BLK * (HD + width) * 2,
        ),
    )(step_size, flat_lists, weights, kv_rows)


def per_device(queries, keys, values, key_lists, counts, *, x_count):
    group = ("y", "core", "x")
    pb_count = lax.axis_size("y") * lax.axis_size("core")
    z_count = lax.axis_size("z")
    group_count = pb_count * x_count
    kv_count = z_count * x_count
    assert HEADS == group_count
    tokens = keys.shape[0]
    assert BLK == x_count * tokens
    rows = queries.shape[0]
    per_dev = rows // BLK
    meta_width = per_dev * (MOST + 1)
    meta_rows = 16
    assert meta_width <= HD

    kv_heads = jnp.concatenate(
        [
            keys.reshape(tokens, HEADS, HD).transpose(1, 0, 2),
            values.reshape(tokens, HEADS, HD).transpose(1, 0, 2),
        ],
        axis=2,
    )
    kv_split = lax.all_to_all(kv_heads, group, split_axis=0, concat_axis=0, tiled=True)
    kv_part = kv_split.reshape(group_count * tokens, 2 * HD)
    kv_rows = lax.all_gather(kv_part, "z", axis=0, tiled=True)

    kv_index = lax.axis_index("z") * x_count + lax.axis_index("x")
    own_lists = lax.dynamic_slice_in_dim(key_lists, kv_index * per_dev, per_dev, axis=0)
    own_counts = lax.dynamic_slice_in_dim(counts, kv_index * per_dev, per_dev, axis=0)
    meta = jnp.concatenate([own_lists, own_counts[:, None]], axis=1).reshape(-1)
    meta_block = jnp.zeros((meta_rows, HD), jnp.bfloat16).at[0, :meta_width].set(
        meta.astype(jnp.bfloat16)
    )
    q_heads = jnp.concatenate(
        [
            queries.reshape(rows, HEADS, HD).transpose(1, 0, 2),
            jnp.broadcast_to(meta_block[None], (HEADS, meta_rows, HD)),
        ],
        axis=1,
    )
    q_src = lax.all_to_all(q_heads, group, split_axis=0, concat_axis=0, tiled=True)

    meta_in = q_src[:, rows, :meta_width].astype(jnp.int32)
    meta_in = meta_in.reshape(group_count * per_dev, MOST + 1)
    lists = meta_in[:, :MOST]
    lists = (lists % z_count) * pb_count + lists // z_count
    local_counts = meta_in[:, MOST]

    produced = attend(q_src, kv_rows, lists, local_counts, per_dev)
    back = lax.all_to_all(
        produced.reshape(group_count, rows, HD), group, split_axis=0, concat_axis=0, tiled=True
    )
    return back.transpose(1, 0, 2).reshape(queries.shape)


def solution(mesh):
    pb_count, kv_count = mesh.shape["pb"], mesh.shape["kv"]
    x_count = 4
    fine = jax.sharding.Mesh(
        mesh.devices.reshape(pb_count // 2, 2, kv_count // x_count, x_count),
        ("y", "core", "z", "x"),
    )
    rows = P(("y", "core", "z", "x"), None)
    return jax.shard_map(
        functools.partial(per_device, x_count=x_count),
        mesh=fine,
        in_specs=(rows, rows, rows, P(("y", "core"), None), P(("y", "core"))),
        out_specs=rows,
        check_vma=False,
    )
```

```python
import functools

import jax
import jax.numpy as jnp
from jax import lax
from jax.experimental import pallas as pl
from jax.experimental.pallas import tpu as pltpu
from jax.sharding import PartitionSpec as P

HEADS = 32
HD = 128
BLK = 128
MOST = 8


SLOT_SIZES = (2, 3, 4, 5, 6, 7, MOST)


def weights_kernel(step_ref, lists_ref, counts_ref, q_ref, k_ref, w_ref, kc_ref,
                   *, per_step, per_dev, scaling):
    step = pl.program_id(0)

    def body_for(slots):
        def body():
            for i in range(per_step):
                qb = step * per_step + i
                cnt = counts_ref[qb]
                q = q_ref[i // per_dev, pl.ds((i % per_dev) * BLK, BLK), :]
                for s in range(slots):
                    kb = lists_ref[qb * MOST + s]
                    start = pl.multiple_of(kb * BLK, BLK)
                    kc_ref[pl.ds(s * BLK, BLK), :] = k_ref[pl.ds(start, BLK), :]
                sc = lax.dot_general(q, kc_ref[pl.ds(0, slots * BLK), :], (((1,), (1,)), ((), ())),
                                     preferred_element_type=jnp.float32) * scaling
                slot = lax.broadcasted_iota(jnp.int32, sc.shape, 1) // BLK
                sc = jnp.where(slot < cnt, sc, -jnp.inf)
                m = jnp.max(sc, axis=-1, keepdims=True)
                p = jnp.exp(sc - m)
                l = jnp.sum(p, axis=-1, keepdims=True)
                w_ref[i, :, pl.ds(0, slots * BLK)] = (p / l).astype(jnp.bfloat16)
        return body

    lax.switch(step_ref[step], [body_for(n) for n in SLOT_SIZES])


def mix_kernel(step_ref, lists_ref, w_ref, v_ref, o_ref, vc_ref, *, per_step):
    step = pl.program_id(0)

    def body_for(slots):
        def body():
            for i in range(per_step):
                qb = step * per_step + i
                for s in range(slots):
                    kb = lists_ref[qb * MOST + s]
                    start = pl.multiple_of(kb * BLK, BLK)
                    vc_ref[pl.ds(s * BLK, BLK), :] = v_ref[pl.ds(start, BLK), :]
                w = w_ref[i, :, pl.ds(0, slots * BLK)]
                out = jnp.dot(w, vc_ref[pl.ds(0, slots * BLK), :],
                              preferred_element_type=jnp.float32)
                o_ref[i] = out.astype(o_ref.dtype)
        return body

    lax.switch(step_ref[step], [body_for(n) for n in SLOT_SIZES])


def attend(q_src, kv_rows, lists, counts, per_dev):
    sources = q_src.shape[0]
    blocks = sources * per_dev
    per_src = 8 if sources % 8 == 0 else 1
    per_step = per_src * per_dev
    nk = kv_rows.shape[0]
    width = MOST * BLK
    widest = jnp.max(counts.reshape(blocks // per_step, per_step), axis=1)
    step_size = jnp.zeros_like(widest)
    for n in SLOT_SIZES[:-1]:
        step_size = step_size + (widest > n).astype(jnp.int32)
    flat_lists = lists.reshape(-1)
    weights = pl.pallas_call(
        functools.partial(weights_kernel, per_step=per_step, per_dev=per_dev,
                          scaling=HD ** (-0.5)),
        grid_spec=pltpu.PrefetchScalarGridSpec(
            num_scalar_prefetch=3,
            grid=(blocks // per_step,),
            in_specs=[
                pl.BlockSpec((per_src, per_dev * BLK, HD), lambda b, *_: (b, 0, 0)),
                pl.BlockSpec((nk, HD), lambda b, *_: (0, 0)),
            ],
            out_specs=pl.BlockSpec((per_step, BLK, width), lambda b, *_: (b, 0, 0)),
            scratch_shapes=[pltpu.VMEM((width, HD), jnp.bfloat16)],
        ),
        out_shape=jax.ShapeDtypeStruct((blocks, BLK, width), jnp.bfloat16),
        compiler_params=pltpu.CompilerParams(dimension_semantics=("arbitrary",)),
        cost_estimate=pl.CostEstimate(
            flops=blocks * 2 * BLK * width * HD,
            transcendentals=blocks * BLK * width,
            bytes_accessed=kv_rows.size + blocks * BLK * (HD + width) * 2,
        ),
    )(step_size, flat_lists, counts, q_src, kv_rows)
    return pl.pallas_call(
        functools.partial(mix_kernel, per_step=per_step),
        grid_spec=pltpu.PrefetchScalarGridSpec(
            num_scalar_prefetch=2,
            grid=(blocks // per_step,),
            in_specs=[
                pl.BlockSpec((per_step, BLK, width), lambda b, *_: (b, 0, 0)),
                pl.BlockSpec((nk, HD), lambda b, *_: (0, 1)),
            ],
            out_specs=pl.BlockSpec((per_step, BLK, HD), lambda b, *_: (b, 0, 0)),
            scratch_shapes=[pltpu.VMEM((width, HD), jnp.bfloat16)],
        ),
        out_shape=jax.ShapeDtypeStruct((blocks, BLK, HD), jnp.bfloat16),
        compiler_params=pltpu.CompilerParams(dimension_semantics=("arbitrary",)),
        cost_estimate=pl.CostEstimate(
            flops=blocks * 2 * BLK * width * HD,
            transcendentals=0,
            bytes_accessed=kv_rows.size + blocks * BLK * (HD + width) * 2,
        ),
    )(step_size, flat_lists, weights, kv_rows)


def per_device(queries, keys, values, key_lists, counts, *, x_count):
    group = ("y", "core", "x")
    pb_count = lax.axis_size("y") * lax.axis_size("core")
    z_count = lax.axis_size("z")
    group_count = pb_count * x_count
    kv_count = z_count * x_count
    assert HEADS == group_count
    tokens = keys.shape[0]
    assert BLK == x_count * tokens
    rows = queries.shape[0]
    per_dev = rows // BLK
    meta_width = per_dev * (MOST + 1)
    meta_rows = 16
    assert meta_width <= HD

    kv_heads = jnp.concatenate(
        [
            keys.reshape(tokens, HEADS, HD).transpose(1, 0, 2),
            values.reshape(tokens, HEADS, HD).transpose(1, 0, 2),
        ],
        axis=2,
    )
    kv_split = lax.all_to_all(kv_heads, group, split_axis=0, concat_axis=0, tiled=True)
    kv_part = kv_split.reshape(group_count * tokens, 2 * HD)
    kv_rows = lax.all_gather(kv_part, "z", axis=0, tiled=True)

    kv_index = lax.axis_index("z") * x_count + lax.axis_index("x")
    own_lists = lax.dynamic_slice_in_dim(key_lists, kv_index * per_dev, per_dev, axis=0)
    own_counts = lax.dynamic_slice_in_dim(counts, kv_index * per_dev, per_dev, axis=0)
    meta = jnp.concatenate([own_lists, own_counts[:, None]], axis=1).reshape(-1)
    meta_block = jnp.zeros((meta_rows, HD), jnp.bfloat16).at[0, :meta_width].set(
        meta.astype(jnp.bfloat16)
    )
    q_heads = jnp.concatenate(
        [
            queries.reshape(rows, HEADS, HD).transpose(1, 0, 2),
            jnp.broadcast_to(meta_block[None], (HEADS, meta_rows, HD)),
        ],
        axis=1,
    )
    q_src = lax.all_to_all(q_heads, group, split_axis=0, concat_axis=0, tiled=True)

    meta_in = q_src[:, rows, :meta_width].astype(jnp.int32)
    meta_in = meta_in.reshape(group_count * per_dev, MOST + 1)
    lists = meta_in[:, :MOST]
    lists = (lists % z_count) * pb_count + lists // z_count
    local_counts = meta_in[:, MOST]

    produced = attend(q_src, kv_rows, lists, local_counts, per_dev)
    back = lax.all_to_all(
        produced.reshape(group_count, rows, HD), group, split_axis=0, concat_axis=0, tiled=True
    )
    return back.transpose(1, 0, 2).reshape(queries.shape)


def solution(mesh):
    pb_count, kv_count = mesh.shape["pb"], mesh.shape["kv"]
    x_count = 4
    fine = jax.sharding.Mesh(
        mesh.devices.reshape(pb_count // 2, 2, kv_count // x_count, x_count),
        ("y", "core", "z", "x"),
    )
    rows = P(("y", "core", "z", "x"), None)
    return jax.shard_map(
        functools.partial(per_device, x_count=x_count),
        mesh=fine,
        in_specs=(rows, rows, rows, P(("y", "core"), None), P(("y", "core"))),
        out_specs=rows,
        check_vma=False,
    )
```

```python
import functools

import jax
import jax.numpy as jnp
from jax import lax
from jax.experimental import pallas as pl
from jax.experimental.pallas import tpu as pltpu
from jax.sharding import PartitionSpec as P

HEADS = 32
HD = 128
BLK = 128
MOST = 8


SLOT_SIZES = (2, 3, 4, 5, 6, 7, MOST)


def weights_kernel(step_ref, lists_ref, counts_ref, q_ref, k_ref, w_ref, kc_ref,
                   *, per_step, per_dev, scaling):
    step = pl.program_id(0)

    def body_for(slots):
        def body():
            for i in range(per_step):
                qb = step * per_step + i
                cnt = counts_ref[qb]
                q = q_ref[i // per_dev, pl.ds((i % per_dev) * BLK, BLK), :]
                for s in range(slots):
                    kb = lists_ref[qb * MOST + s]
                    start = pl.multiple_of(kb * BLK, BLK)
                    kc_ref[pl.ds(s * BLK, BLK), :] = k_ref[pl.ds(start, BLK), :]
                sc = lax.dot_general(q, kc_ref[pl.ds(0, slots * BLK), :], (((1,), (1,)), ((), ())),
                                     preferred_element_type=jnp.float32) * scaling
                slot = lax.broadcasted_iota(jnp.int32, sc.shape, 1) // BLK
                sc = jnp.where(slot < cnt, sc, -jnp.inf)
                m = jnp.max(sc, axis=-1, keepdims=True)
                p = jnp.exp(sc - m)
                l = jnp.sum(p, axis=-1, keepdims=True)
                w_ref[i, :, pl.ds(0, slots * BLK)] = (p / l).astype(jnp.bfloat16)
        return body

    lax.switch(step_ref[step], [body_for(n) for n in SLOT_SIZES])


def mix_kernel(step_ref, lists_ref, w_ref, v_ref, o_ref, vc_ref, *, per_step):
    step = pl.program_id(0)

    def body_for(slots):
        def body():
            for i in range(per_step):
                qb = step * per_step + i
                for s in range(slots):
                    kb = lists_ref[qb * MOST + s]
                    start = pl.multiple_of(kb * BLK, BLK)
                    vc_ref[pl.ds(s * BLK, BLK), :] = v_ref[pl.ds(start, BLK), :]
                w = w_ref[i, :, pl.ds(0, slots * BLK)]
                out = jnp.dot(w, vc_ref[pl.ds(0, slots * BLK), :],
                              preferred_element_type=jnp.float32)
                o_ref[i] = out.astype(o_ref.dtype)
        return body

    lax.switch(step_ref[step], [body_for(n) for n in SLOT_SIZES])


def attend(q_src, kv_rows, lists, counts, per_dev):
    sources = q_src.shape[0]
    blocks = sources * per_dev
    per_src = 4 if sources % 4 == 0 else 1
    per_step = per_src * per_dev
    nk = kv_rows.shape[1]
    width = MOST * BLK
    widest = jnp.max(counts.reshape(blocks // per_step, per_step), axis=1)
    step_size = jnp.zeros_like(widest)
    for n in SLOT_SIZES[:-1]:
        step_size = step_size + (widest > n).astype(jnp.int32)
    flat_lists = lists.reshape(-1)
    weights = pl.pallas_call(
        functools.partial(weights_kernel, per_step=per_step, per_dev=per_dev,
                          scaling=HD ** (-0.5)),
        grid_spec=pltpu.PrefetchScalarGridSpec(
            num_scalar_prefetch=3,
            grid=(blocks // per_step,),
            in_specs=[
                pl.BlockSpec((per_src, per_dev * BLK, HD), lambda b, *_: (b, 0, 0)),
                pl.BlockSpec((None, nk, HD), lambda b, *_: (0, 0, 0)),
            ],
            out_specs=pl.BlockSpec((per_step, BLK, width), lambda b, *_: (b, 0, 0)),
            scratch_shapes=[pltpu.VMEM((width, HD), jnp.bfloat16)],
        ),
        out_shape=jax.ShapeDtypeStruct((blocks, BLK, width), jnp.bfloat16),
        compiler_params=pltpu.CompilerParams(dimension_semantics=("arbitrary",)),
        cost_estimate=pl.CostEstimate(
            flops=blocks * 2 * BLK * width * HD,
            transcendentals=blocks * BLK * width,
            bytes_accessed=kv_rows.size + blocks * BLK * (HD + width) * 2,
        ),
    )(step_size, flat_lists, counts, q_src, kv_rows)
    return pl.pallas_call(
        functools.partial(mix_kernel, per_step=per_step),
        grid_spec=pltpu.PrefetchScalarGridSpec(
            num_scalar_prefetch=2,
            grid=(blocks // per_step,),
            in_specs=[
                pl.BlockSpec((per_step, BLK, width), lambda b, *_: (b, 0, 0)),
                pl.BlockSpec((None, nk, HD), lambda b, *_: (1, 0, 0)),
            ],
            out_specs=pl.BlockSpec((per_step, BLK, HD), lambda b, *_: (b, 0, 0)),
            scratch_shapes=[pltpu.VMEM((width, HD), jnp.bfloat16)],
        ),
        out_shape=jax.ShapeDtypeStruct((blocks, BLK, HD), jnp.bfloat16),
        compiler_params=pltpu.CompilerParams(dimension_semantics=("arbitrary",)),
        cost_estimate=pl.CostEstimate(
            flops=blocks * 2 * BLK * width * HD,
            transcendentals=0,
            bytes_accessed=kv_rows.size + blocks * BLK * (HD + width) * 2,
        ),
    )(step_size, flat_lists, weights, kv_rows)


def per_device(queries, keys, values, key_lists, counts, *, x_count):
    group = ("y", "core", "x")
    pb_count = lax.axis_size("y") * lax.axis_size("core")
    z_count = lax.axis_size("z")
    group_count = pb_count * x_count
    kv_count = z_count * x_count
    assert HEADS == group_count
    tokens = keys.shape[0]
    assert BLK == x_count * tokens
    rows = queries.shape[0]
    per_dev = rows // BLK
    meta_width = per_dev * (MOST + 1)
    meta_rows = 16
    assert meta_width <= HD

    kv_heads = jnp.concatenate(
        [
            keys.reshape(tokens, HEADS, HD).transpose(1, 0, 2),
            values.reshape(tokens, HEADS, HD).transpose(1, 0, 2),
        ],
        axis=2,
    )
    kv_split = lax.all_to_all(kv_heads, group, split_axis=0, concat_axis=0, tiled=True)
    kv_part = kv_split.reshape(group_count * tokens, 2 * HD)
    kv_planes = kv_part.reshape(group_count * tokens, 2, HD).transpose(1, 0, 2)
    kv_rows = lax.all_gather(kv_planes, "z", axis=1, tiled=True)

    kv_index = lax.axis_index("z") * x_count + lax.axis_index("x")
    own_lists = lax.dynamic_slice_in_dim(key_lists, kv_index * per_dev, per_dev, axis=0)
    own_counts = lax.dynamic_slice_in_dim(counts, kv_index * per_dev, per_dev, axis=0)
    meta = jnp.concatenate([own_lists, own_counts[:, None]], axis=1).reshape(-1)
    meta_block = jnp.zeros((meta_rows, HD), jnp.bfloat16).at[0, :meta_width].set(
        meta.astype(jnp.bfloat16)
    )
    q_heads = jnp.concatenate(
        [
            queries.reshape(rows, HEADS, HD).transpose(1, 0, 2),
            jnp.broadcast_to(meta_block[None], (HEADS, meta_rows, HD)),
        ],
        axis=1,
    )
    q_src = lax.all_to_all(q_heads, group, split_axis=0, concat_axis=0, tiled=True)

    meta_in = q_src[:, rows, :meta_width].astype(jnp.int32)
    meta_in = meta_in.reshape(group_count * per_dev, MOST + 1)
    lists = meta_in[:, :MOST]
    lists = (lists % z_count) * pb_count + lists // z_count
    local_counts = meta_in[:, MOST]

    produced = attend(q_src, kv_rows, lists, local_counts, per_dev)
    back = lax.all_to_all(
        produced.reshape(group_count, rows, HD), group, split_axis=0, concat_axis=0, tiled=True
    )
    return back.transpose(1, 0, 2).reshape(queries.shape)


def solution(mesh):
    pb_count, kv_count = mesh.shape["pb"], mesh.shape["kv"]
    x_count = 4
    fine = jax.sharding.Mesh(
        mesh.devices.reshape(pb_count // 2, 2, kv_count // x_count, x_count),
        ("y", "core", "z", "x"),
    )
    rows = P(("y", "core", "z", "x"), None)
    return jax.shard_map(
        functools.partial(per_device, x_count=x_count),
        mesh=fine,
        in_specs=(rows, rows, rows, P(("y", "core"), None), P(("y", "core"))),
        out_specs=rows,
        check_vma=False,
    )
```
